256 devices in a mesh: owner: 8 (over z_hi, x), ctx: 32 (over y, z_lo, core).
Axes of the slice: x: 4, y: 4, z: 8 (z_hi: 2, z_lo: 4; z = z_hi * 4 + z_lo), core: 2. Of those that a mesh axis runs over, the one named last changes fastest.
Arguments:
- span_cache: bfloat16 [2048, 128, 1024], P(('owner', 'ctx')), may hold values from -8 to 8
- retrieval: int32 [8, 256], P(None, 'ctx'), may hold values from 0 to 2047, as said below
- counts: int32 [8], replicated, may hold values from 64 to 256, as said below
- recompute_pos: int32 [8, 256], P('owner'), may hold values from 0 to 1023, as said below
- hidden: bfloat16 [8, 256, 8192], P('owner', None, 'ctx'), may hold values from -6 to 6
- kv_weight: bfloat16 [8192, 1024], P('ctx'), may hold values from -0.0625 to 0.0625
- queries: bfloat16 [8, 256, 4096], P('owner', 'ctx'), may hold values from -8 to 8
- block_mask: int32 [8, 256, 256], P('owner', None, 'ctx'), may hold values from 0 to 1, as said below
Outputs:
- context_kv: bfloat16 [8, 32768, 1024], P('owner', 'ctx')
- attended: bfloat16 [8, 256, 4096], P('owner', 'ctx')
The draws below stay inside these ranges and needn't reach their ends.
Inputs may be any that keep to these rules, and one draw needn't show every extreme that they name: `retrieval`: the span for block b of a request is stored on index b // 8 of ctx of some owner group o: its number is (o * 32 + b // 8) * 8 + s. Among the 8 blocks of one request on one index of ctx at most 4 name spans of one owner group, and in every draw some reach 4. `counts`: some request uses all 256 blocks in every draw. `recompute_pos`: the 8 positions of one request on one index of ctx are distinct. `block_mask`: every query block may see itself and those of the first 4 blocks not after it; no block sees a later one.
All inputs are finite; a program needn't handle non-finite values.
Results may differ from the reference program's by a relative error of at most 0.023.
Values may be sent and summed in bfloat16 or wider, within the bound.
No kernel may reach another device: no remote copies, remote signals or barrier semaphores. Data moves between devices by JAX's collectives and lax.ppermute only.
A program may use at most 128 MiB of HBM per device.

```python
import jax
import jax.numpy as jnp
from jax import lax

D = 8192
QH = 32
KVH = 4
HD = 128
BLK = 128
NBD = 8
RCP = 8
SLOTS = 8
CAP = 4
PREFIX = 4
CTX_DEV = 1024
NB = 256
SEQ = 32768
REQS = 8
SPANS = 2048
NQ = 256
KVW = 1024
N_OWNER = 8
N_CTX = 32


def draw_span_cache(key, part):
    key_body = jax.random.fold_in(jax.random.fold_in(key, 11), 0)
    shape = (SPANS, BLK, 2 * KVH * HD)
    drawn = jnp.clip(jax.random.normal(key_body, shape, jnp.float32), -5.0, 5.0)
    return drawn.astype(jnp.bfloat16)


def draw_queries(key, part):
    key_body = jax.random.fold_in(jax.random.fold_in(key, 23), 0)
    shape = (REQS, NQ, QH * HD)
    drawn = jnp.clip(jax.random.normal(key_body, shape, jnp.float32), -5.0, 5.0)
    return drawn.astype(jnp.bfloat16)


def draw_retrieval(key, part):
    key_perm, key_jitter, key_slot, key_shuffle = jax.random.split(jax.random.fold_in(key, 31), 4)
    contender_total = N_OWNER * CAP
    heat_order = jax.random.permutation(key_perm, N_OWNER)
    demand_ordinal_position = jnp.zeros((N_OWNER,), jnp.int32).at[heat_order].set(jnp.arange(N_OWNER, dtype=jnp.int32))
    contender_holder_device = jnp.repeat(jnp.arange(N_OWNER, dtype=jnp.int32), CAP)
    stochastic_jitter = jax.random.randint(key_jitter, (REQS, N_CTX, contender_total), 0, 1024)
    demand_increment = (N_OWNER - demand_ordinal_position[contender_holder_device]) * 160
    mandated_selection = jnp.where((jnp.arange(N_CTX) == 0)[:, None] & (demand_ordinal_position[contender_holder_device] == 0)[None, :], 100000, 0)
    precedence_sequence = (stochastic_jitter + demand_increment[None, None, :] + mandated_selection[None, :, :]) * contender_total + jnp.arange(contender_total, dtype=jnp.int32)
    picked = jnp.argsort(-precedence_sequence, axis=-1)[..., :NBD]
    owners_drawn = contender_holder_device[picked]
    shuffle_keys = jax.random.randint(key_shuffle, (REQS, N_CTX, NBD), 0, 1 << 20) * NBD + jnp.arange(NBD, dtype=jnp.int32)
    shuffle = jnp.argsort(shuffle_keys, axis=-1)
    owners_drawn = jnp.take_along_axis(owners_drawn, shuffle, axis=-1)
    slot_draw = jax.random.randint(key_slot, (REQS, N_CTX, NBD), 0, SLOTS)
    span_ids = (owners_drawn * N_CTX + jnp.arange(N_CTX, dtype=jnp.int32)[None, :, None]) * SLOTS + slot_draw
    return span_ids.reshape(REQS, N_CTX * NBD).astype(jnp.int32)


def draw_counts(key, part):
    lower = max(PREFIX + 1, NB // 4)
    drawn = jax.random.randint(jax.random.fold_in(key, 41), (REQS,), lower, NB + 1)
    full_request = jax.random.randint(jax.random.fold_in(key, 43), (), 0, REQS)
    return jnp.where(jnp.arange(REQS) == full_request, NB, drawn).astype(jnp.int32)


def draw_recompute_pos(key, part):
    precedence_sequence = jax.random.randint(jax.random.fold_in(key, 53), (REQS, N_CTX, CTX_DEV), 0, 1 << 20) * CTX_DEV + jnp.arange(CTX_DEV, dtype=jnp.int32)
    picked = jnp.argsort(precedence_sequence, axis=-1)[..., :RCP]
    return picked.reshape(REQS, N_CTX * RCP).astype(jnp.int32)


def draw_block_mask(key, part):
    query_block = jnp.arange(NB, dtype=jnp.int32)[:, None]
    key_block = jnp.arange(NB, dtype=jnp.int32)[None, :]
    extra = jax.random.randint(jax.random.fold_in(key, 61), (REQS, NB, NB), 0, 8) == 0
    allowed = (key_block < PREFIX) | (key_block == query_block) | extra & (key_block < query_block)
    allowed = allowed & (key_block <= query_block)
    return allowed.astype(jnp.int32)


def steps_of(stream_key, dims, cuts, low, largest):
    level, own = 1.0, jax.random.fold_in(stream_key, 6)
    for dim, parts in cuts:
        heights = jnp.exp(jax.random.uniform(jax.random.fold_in(own, dim), (parts,), jnp.float32, low / len(cuts), largest / len(cuts)))
        level = level * jnp.repeat(heights, dims[dim] // parts).reshape([-1 if axis == dim else 1 for axis in range(len(dims))])
    return level


def centred(rng, shape, deviation, bound, pieces=(), held_as=jnp.bfloat16):
    entries = jax.random.normal(rng, shape, jnp.float32) * deviation
    if len(pieces) > 0:
        entries = steps_of(rng, shape, pieces, -0.22, 0.18) * entries
    return jnp.clip(entries, min=-bound, max=bound).astype(held_as)


def setup_inputs(seed: int = 0) -> dict:
    seeds = jax.random.split(jax.random.key(seed), 9)
    span_cache = draw_span_cache(jax.random.fold_in(seeds[8], 71), 0)
    retrieval = draw_retrieval(jax.random.fold_in(seeds[8], 71), 0)
    counts = draw_counts(jax.random.fold_in(seeds[8], 71), 0)
    recompute_pos = draw_recompute_pos(jax.random.fold_in(seeds[8], 71), 0)
    hidden = centred(seeds[4], (REQS, NQ, D), 1.0, 6.0, ((0, 8), (2, 32)))
    kv_weight = centred(seeds[5], (D, KVW), D ** -0.5, 0.0625, ((0, 32),))
    queries = draw_queries(jax.random.fold_in(seeds[8], 71), 0)
    block_mask = draw_block_mask(jax.random.fold_in(seeds[8], 71), 0)
    return dict(span_cache=span_cache, retrieval=retrieval, counts=counts, recompute_pos=recompute_pos, hidden=hidden, kv_weight=kv_weight, queries=queries, block_mask=block_mask)


def attend_request(query_rows, context_rows, query_pos, mask_rows, request_count):
    key_pos = jnp.arange(SEQ, dtype=jnp.int32)
    key_block = key_pos // BLK
    allowed = jnp.take(mask_rows, query_pos // BLK, axis=0)
    visible = jnp.repeat(allowed, BLK, axis=1) > 0
    visible = visible & (key_block[None, :] < request_count) & (key_pos[None, :] <= query_pos[:, None])
    key_rows = context_rows[:, :KVH * HD].astype(jnp.float32)
    value_rows = context_rows[:, KVH * HD:].astype(jnp.float32)
    query_float = query_rows.astype(jnp.float32)
    per_group = QH // KVH
    scaling = HD ** -0.5

    def one_head(head_index):
        kv_index = head_index // per_group
        query_head = lax.dynamic_slice_in_dim(query_float, head_index * HD, HD, 1)
        key_head = lax.dynamic_slice_in_dim(key_rows, kv_index * HD, HD, 1)
        value_head = lax.dynamic_slice_in_dim(value_rows, kv_index * HD, HD, 1)
        scores = jnp.dot(query_head, key_head.T, precision=lax.Precision.HIGHEST) * scaling
        scores = jnp.where(visible, scores, -1e30)
        highest = jnp.max(scores, axis=1, keepdims=True)
        weights = jnp.where(visible, jnp.exp(scores - highest), 0.0)
        weight_sum = jnp.sum(weights, axis=1, keepdims=True)
        rounded = lax.optimization_barrier(weights.astype(jnp.bfloat16)).astype(jnp.float32)
        numerator = jnp.dot(rounded, value_head, precision=lax.Precision.HIGHEST)
        return numerator / weight_sum

    per_head = lax.map(one_head, jnp.arange(QH, dtype=jnp.int32))
    return jnp.transpose(per_head, (1, 0, 2)).reshape(NQ, QH * HD).astype(jnp.bfloat16)


def reference(span_cache, retrieval, counts, recompute_pos, hidden, kv_weight, queries, block_mask):
    in_use = jnp.arange(NB, dtype=jnp.int32)[None, :] < counts[:, None]

    def build_request(request):
        span_ids = retrieval[request]
        blocks = jnp.take(span_cache, span_ids, axis=0)
        blocks = jnp.where(in_use[request][:, None, None], blocks, jnp.zeros_like(blocks))
        context_rows = blocks.reshape(SEQ, KVW)
        recomputed = jnp.dot(hidden[request], kv_weight, preferred_element_type=jnp.float32).astype(jnp.bfloat16)
        query_pos = (jnp.arange(NQ, dtype=jnp.int32) // RCP) * CTX_DEV + recompute_pos[request]
        context_rows = context_rows.at[query_pos].set(recomputed)
        attended = attend_request(queries[request], context_rows, query_pos, block_mask[request], counts[request])
        return context_rows, attended

    context_kv, attended = lax.map(build_request, jnp.arange(REQS, dtype=jnp.int32))
    return context_kv, attended
```

```python
import jax
import jax.numpy as jnp
from jax import lax
from jax.sharding import PartitionSpec as P

QH = 32
KVH = 4
HD = 128
BLK = 128
NBD = 8
RCP = 8
SLOTS = 8
CAP = 4
CTX_DEV = 1024


def on_device(span_cache, retrieval, counts, recompute_pos, hidden, kv_weight, queries, block_mask):
    owner_count = lax.axis_size("owner")
    cycle_size = lax.axis_size("ctx")
    my_owner = lax.axis_index("owner")
    my_ctx = lax.axis_index("ctx")
    feature_count = span_cache.shape[2]
    positions = jnp.arange(NBD, dtype=jnp.int32)
    block_ids = my_ctx * NBD + positions
    in_use = block_ids[None, :] < counts[:, None]
    holder = retrieval // (cycle_size * SLOTS)
    outbound = in_use & (holder == my_owner)
    slot_rank = jnp.cumsum(outbound.astype(jnp.int32), axis=1) - 1
    picked = outbound[:, None, :] & (
        slot_rank[:, None, :] == jnp.arange(CAP, dtype=jnp.int32)[None, :, None]
    )
    chosen = jnp.sum(jnp.where(picked, (retrieval % SLOTS)[:, None, :], 0), axis=2)
    filled = jnp.any(picked, axis=2)
    outgoing = jnp.where(
        filled[:, :, None, None], jnp.take(span_cache, chosen, axis=0), jnp.zeros((), jnp.bfloat16)
    )
    arrived = lax.all_to_all(outgoing, "owner", split_axis=0, concat_axis=0, tiled=True)
    wanted = lax.dynamic_index_in_dim(retrieval, my_owner, 0, keepdims=False)
    my_count = lax.dynamic_index_in_dim(counts, my_owner, 0, keepdims=False)
    my_in_use = block_ids < my_count
    source = wanted // (cycle_size * SLOTS)
    earlier = (
        (source[:, None] == source[None, :])
        & my_in_use[None, :]
        & (positions[None, :] < positions[:, None])
    )
    ordinal = jnp.sum(earlier.astype(jnp.int32), axis=1)
    flattened = arrived.reshape(owner_count * CAP, BLK, feature_count)
    blocks = jnp.take(flattened, source * CAP + ordinal, axis=0, mode="clip")
    blocks = jnp.where(my_in_use[:, None, None], blocks, jnp.zeros((), jnp.bfloat16))
    context = blocks.reshape(CTX_DEV, feature_count)
    local_rows = hidden[0]
    recomputed = lax.psum_scatter(
        jnp.dot(local_rows, kv_weight, preferred_element_type=jnp.float32).astype(jnp.bfloat16),
        "ctx",
        scatter_dimension=0,
        tiled=True,
    )
    every_pos = recompute_pos[0]
    own_pos = lax.dynamic_slice_in_dim(every_pos, my_ctx * RCP, RCP)
    matches = jnp.arange(CTX_DEV, dtype=jnp.int32)[:, None] == own_pos[None, :]
    placed = jnp.dot(
        matches.astype(jnp.bfloat16), recomputed, preferred_element_type=jnp.float32
    ).astype(jnp.bfloat16)
    context = jnp.where(jnp.any(matches, axis=1)[:, None], placed, context)
    key_width = KVH * HD
    key_rows = context[:, :key_width].reshape(CTX_DEV, KVH, HD)
    value_rows = context[:, key_width:].reshape(CTX_DEV, KVH, HD)
    key_pos = my_ctx * CTX_DEV + jnp.arange(CTX_DEV, dtype=jnp.int32)
    key_in_use = key_pos // BLK < my_count
    mask_cols = block_mask[0]
    query_count = cycle_size * RCP
    query_pos = jnp.arange(query_count, dtype=jnp.int32) // RCP * CTX_DEV + every_pos
    all_queries = lax.all_gather(queries[0], "ctx", axis=0, tiled=True)
    per_group = QH // KVH
    allowed = jnp.take(mask_cols, query_pos // BLK, axis=0)
    visible = jnp.repeat(allowed, BLK, axis=1) > 0
    visible = visible & key_in_use[None, :] & (key_pos[None, :] <= query_pos[:, None])
    grouped = all_queries.reshape(query_count, KVH, per_group, HD)
    scores = jnp.einsum(
        "rkgd,tkd->kgrt", grouped, key_rows, preferred_element_type=jnp.float32
    ) * HD ** (-0.5)
    scores = jnp.where(visible[None, None], scores, -1e30)
    local_max = jnp.max(scores, axis=3)
    weights = jnp.where(visible[None, None], jnp.exp(scores - local_max[..., None]), 0.0)
    local_sum = jnp.sum(weights, axis=3)
    weighted = jnp.einsum(
        "kgrt,tkd->rkgd",
        weights.astype(jnp.bfloat16),
        value_rows,
        preferred_element_type=jnp.float32,
    )
    global_max = lax.pmax(local_max, "ctx")
    factor = jnp.exp(local_max - global_max)
    numerator = weighted * jnp.transpose(factor, (2, 0, 1))[..., None]
    totals = jnp.transpose(local_sum * factor, (2, 0, 1)).reshape(query_count, QH)
    reduced = lax.psum_scatter(numerator.reshape(query_count, QH * HD), "ctx", scatter_dimension=0, tiled=True)
    reduced_totals = lax.psum_scatter(totals, "ctx", scatter_dimension=0, tiled=True)
    result = reduced.reshape(RCP, QH, HD) / reduced_totals[:, :, None]
    attended = result.reshape(RCP, QH * HD).astype(jnp.bfloat16)
    return (context[None], attended[None])


def solution(mesh):
    in_specs = (
        P(("owner", "ctx"), None, None),
        P(None, "ctx"),
        P(),
        P("owner", None),
        P("owner", None, "ctx"),
        P("ctx", None),
        P("owner", "ctx", None),
        P("owner", None, "ctx"),
    )
    out_specs = (P("owner", "ctx", None), P("owner", "ctx", None))
    return jax.shard_map(
        on_device, mesh=mesh, in_specs=in_specs, out_specs=out_specs, check_vma=False
    )
```

```python
import jax
import jax.numpy as jnp
from jax import lax
from jax.sharding import PartitionSpec as P

QH = 32
KVH = 4
HD = 128
BLK = 128
NBD = 8
RCP = 8
SLOTS = 8
CAP = 4
CTX_DEV = 1024


def exchange(shard, bit):
    peers = lax.axis_size("ctx")
    return lax.ppermute(shard, "ctx", [(i, i ^ bit) for i in range(peers)])


def gather_rows(block, my_ctx):
    peers = lax.axis_size("ctx")
    held = block
    bit = 1
    while bit < peers:
        other = exchange(held, bit)
        upper = (my_ctx // bit) % 2 == 1
        held = jnp.where(
            upper, jnp.concatenate([other, held]), jnp.concatenate([held, other])
        )
        bit *= 2
    return held


def scatter_rows(parts, my_ctx, merge):
    peers = lax.axis_size("ctx")
    held = parts
    bit = 1
    while bit < peers:
        half = jax.tree.map(lambda a: a.reshape((a.shape[0] // 2, 2) + a.shape[1:]), held)
        upper = (my_ctx // bit) % 2 == 1
        keep = jax.tree.map(lambda a: jnp.where(upper, a[:, 1], a[:, 0]), half)
        send = jax.tree.map(lambda a: jnp.where(upper, a[:, 0], a[:, 1]), half)
        held = merge(keep, exchange(send, bit))
        bit *= 2
    return jax.tree.map(lambda a: a[0], held)


def add_parts(a, b):
    return a + b


def merge_softmax(a, b):
    numerator_a, running_a, totals_a = a
    numerator_b, running_b, totals_b = b
    newest = jnp.maximum(running_a, running_b)
    factor_a = jnp.exp(running_a - newest)
    factor_b = jnp.exp(running_b - newest)
    numerator = numerator_a * factor_a[..., None] + numerator_b * factor_b[..., None]
    return (numerator, newest, totals_a * factor_a + totals_b * factor_b)

def on_device(span_cache, retrieval, counts, recompute_pos, hidden, kv_weight, queries, block_mask):
    owner_count = lax.axis_size("owner")
    cycle_size = lax.axis_size("ctx")
    my_owner = lax.axis_index("owner")
    my_ctx = lax.axis_index("ctx")
    feature_count = span_cache.shape[2]
    positions = jnp.arange(NBD, dtype=jnp.int32)
    block_ids = my_ctx * NBD + positions
    in_use = block_ids[None, :] < counts[:, None]
    holder = retrieval // (cycle_size * SLOTS)
    outbound = in_use & (holder == my_owner)
    slot_rank = jnp.cumsum(outbound.astype(jnp.int32), axis=1) - 1
    picked = outbound[:, None, :] & (
        slot_rank[:, None, :] == jnp.arange(CAP, dtype=jnp.int32)[None, :, None]
    )
    chosen = jnp.sum(jnp.where(picked, (retrieval % SLOTS)[:, None, :], 0), axis=2)
    filled = jnp.any(picked, axis=2)
    outgoing = jnp.where(
        filled[:, :, None, None], jnp.take(span_cache, chosen, axis=0), jnp.zeros((), jnp.bfloat16)
    )
    arrived = lax.all_to_all(outgoing, "owner", split_axis=0, concat_axis=0, tiled=True)
    wanted = lax.dynamic_index_in_dim(retrieval, my_owner, 0, keepdims=False)
    my_count = lax.dynamic_index_in_dim(counts, my_owner, 0, keepdims=False)
    my_in_use = block_ids < my_count
    source = wanted // (cycle_size * SLOTS)
    earlier = (
        (source[:, None] == source[None, :])
        & my_in_use[None, :]
        & (positions[None, :] < positions[:, None])
    )
    ordinal = jnp.sum(earlier.astype(jnp.int32), axis=1)
    flattened = arrived.reshape(owner_count * CAP, BLK, feature_count)
    blocks = jnp.take(flattened, source * CAP + ordinal, axis=0, mode="clip")
    blocks = jnp.where(my_in_use[:, None, None], blocks, jnp.zeros((), jnp.bfloat16))
    context = blocks.reshape(CTX_DEV, feature_count)
    local_rows = hidden[0]
    partial = jnp.dot(local_rows, kv_weight, preferred_element_type=jnp.float32)
    recomputed = scatter_rows(
        partial.reshape(cycle_size, RCP, feature_count), my_ctx, add_parts
    ).astype(jnp.bfloat16)
    every_pos = recompute_pos[0]
    own_pos = lax.dynamic_slice_in_dim(every_pos, my_ctx * RCP, RCP)
    matches = jnp.arange(CTX_DEV, dtype=jnp.int32)[:, None] == own_pos[None, :]
    placed = jnp.dot(
        matches.astype(jnp.bfloat16), recomputed, preferred_element_type=jnp.float32
    ).astype(jnp.bfloat16)
    context = jnp.where(jnp.any(matches, axis=1)[:, None], placed, context)
    key_width = KVH * HD
    key_rows = context[:, :key_width].reshape(CTX_DEV, KVH, HD)
    value_rows = context[:, key_width:].reshape(CTX_DEV, KVH, HD)
    key_pos = my_ctx * CTX_DEV + jnp.arange(CTX_DEV, dtype=jnp.int32)
    key_in_use = key_pos // BLK < my_count
    mask_cols = block_mask[0]
    query_count = cycle_size * RCP
    query_pos = jnp.arange(query_count, dtype=jnp.int32) // RCP * CTX_DEV + every_pos
    all_queries = gather_rows(queries[0], my_ctx)
    per_group = QH // KVH
    allowed = jnp.take(mask_cols, query_pos // BLK, axis=0)
    visible = jnp.repeat(allowed, BLK, axis=1) > 0
    visible = visible & key_in_use[None, :] & (key_pos[None, :] <= query_pos[:, None])
    grouped = all_queries.reshape(query_count, KVH, per_group, HD)
    scores = jnp.einsum(
        "rkgd,tkd->kgrt", grouped, key_rows, preferred_element_type=jnp.float32
    ) * HD ** (-0.5)
    scores = jnp.where(visible[None, None], scores, -1e30)
    local_max = jnp.max(scores, axis=3)
    weights = jnp.where(visible[None, None], jnp.exp(scores - local_max[..., None]), 0.0)
    local_sum = jnp.sum(weights, axis=3)
    weighted = jnp.einsum(
        "kgrt,tkd->rkgd",
        weights.astype(jnp.bfloat16),
        value_rows,
        preferred_element_type=jnp.float32,
    )
    running = jnp.transpose(local_max, (2, 0, 1)).reshape(query_count, QH)
    totals = jnp.transpose(local_sum, (2, 0, 1)).reshape(query_count, QH)
    numerator = weighted.reshape(query_count, QH, HD)
    numerator, running, totals = scatter_rows(
        (
            numerator.reshape(cycle_size, RCP, QH, HD),
            running.reshape(cycle_size, RCP, QH),
            totals.reshape(cycle_size, RCP, QH),
        ),
        my_ctx,
        merge_softmax,
    )
    result = numerator / totals[:, :, None]
    attended = result.reshape(RCP, QH * HD).astype(jnp.bfloat16)
    return (context[None], attended[None])


def solution(mesh):
    in_specs = (
        P(("owner", "ctx"), None, None),
        P(None, "ctx"),
        P(),
        P("owner", None),
        P("owner", None, "ctx"),
        P("ctx", None),
        P("owner", "ctx", None),
        P("owner", None, "ctx"),
    )
    out_specs = (P("owner", "ctx", None), P("owner", "ctx", None))
    return jax.shard_map(
        on_device, mesh=mesh, in_specs=in_specs, out_specs=out_specs, check_vma=False
    )
```

```python
import jax
import jax.numpy as jnp
from jax import lax
from jax.sharding import PartitionSpec as P

QH = 32
KVH = 4
HD = 128
BLK = 128
NBD = 8
RCP = 8
SLOTS = 8
CAP = 4
CTX_DEV = 1024


def exchange(shard, bit):
    peers = lax.axis_size("ctx")
    return lax.ppermute(shard, "ctx", [(i, i ^ bit) for i in range(peers)])


def gather_rows(block, my_ctx):
    peers = lax.axis_size("ctx")
    held = block
    bit = 1
    while bit < peers:
        other = exchange(held, bit)
        upper = (my_ctx // bit) % 2 == 1
        held = jnp.where(
            upper, jnp.concatenate([other, held]), jnp.concatenate([held, other])
        )
        bit *= 2
    return held


def scatter_rows(parts, my_ctx, merge):
    peers = lax.axis_size("ctx")
    held = parts
    bit = 1
    while bit < peers:
        half = jax.tree.map(lambda a: a.reshape((a.shape[0] // 2, 2) + a.shape[1:]), held)
        upper = (my_ctx // bit) % 2 == 1
        keep = jax.tree.map(lambda a: jnp.where(upper, a[:, 1], a[:, 0]), half)
        send = jax.tree.map(lambda a: jnp.where(upper, a[:, 0], a[:, 1]), half)
        held = merge(keep, exchange(send, bit))
        bit *= 2
    return jax.tree.map(lambda a: a[0], held)


def add_parts(a, b):
    return a + b


def merge_softmax(a, b):
    numerator_a, running_a, totals_a = a
    numerator_b, running_b, totals_b = b
    newest = jnp.maximum(running_a, running_b)
    factor_a = jnp.exp(running_a - newest)
    factor_b = jnp.exp(running_b - newest)
    numerator = numerator_a * factor_a[..., None] + numerator_b * factor_b[..., None]
    return (numerator, newest, totals_a * factor_a + totals_b * factor_b)

def on_device(span_cache, retrieval, counts, recompute_pos, hidden, kv_weight, queries, block_mask):
    owner_count = lax.axis_size("owner")
    cycle_size = lax.axis_size("ctx")
    my_owner = lax.axis_index("owner")
    my_ctx = lax.axis_index("ctx")
    feature_count = span_cache.shape[2]
    positions = jnp.arange(NBD, dtype=jnp.int32)
    block_ids = my_ctx * NBD + positions
    in_use = block_ids[None, :] < counts[:, None]
    holder = retrieval // (cycle_size * SLOTS)
    outbound = in_use & (holder == my_owner)
    slot_rank = jnp.cumsum(outbound.astype(jnp.int32), axis=1) - 1
    picked = outbound[:, None, :] & (
        slot_rank[:, None, :] == jnp.arange(CAP, dtype=jnp.int32)[None, :, None]
    )
    chosen = jnp.sum(jnp.where(picked, (retrieval % SLOTS)[:, None, :], 0), axis=2)
    filled = jnp.any(picked, axis=2)
    pieces = []
    for shift in range(owner_count):
        target = (my_owner + shift) % owner_count
        chosen_here = lax.dynamic_index_in_dim(chosen, target, 0, keepdims=False)
        filled_here = lax.dynamic_index_in_dim(filled, target, 0, keepdims=False)
        piece = jnp.where(
            filled_here[:, None, None],
            jnp.take(span_cache, chosen_here, axis=0),
            jnp.zeros((), jnp.bfloat16),
        )
        if shift:
            piece = lax.ppermute(
                piece, "owner", [(i, (i + shift) % owner_count) for i in range(owner_count)]
            )
        pieces.append(piece)
    wanted = lax.dynamic_index_in_dim(retrieval, my_owner, 0, keepdims=False)
    my_count = lax.dynamic_index_in_dim(counts, my_owner, 0, keepdims=False)
    my_in_use = block_ids < my_count
    source = wanted // (cycle_size * SLOTS)
    earlier = (
        (source[:, None] == source[None, :])
        & my_in_use[None, :]
        & (positions[None, :] < positions[:, None])
    )
    ordinal = jnp.sum(earlier.astype(jnp.int32), axis=1)
    flattened = jnp.concatenate(pieces, axis=0)
    shift_of_source = (my_owner - source) % owner_count
    blocks = jnp.take(flattened, shift_of_source * CAP + ordinal, axis=0, mode="clip")
    blocks = jnp.where(my_in_use[:, None, None], blocks, jnp.zeros((), jnp.bfloat16))
    context = blocks.reshape(CTX_DEV, feature_count)
    local_rows = hidden[0]
    partial = jnp.dot(local_rows, kv_weight, preferred_element_type=jnp.float32)
    recomputed = scatter_rows(
        partial.reshape(cycle_size, RCP, feature_count), my_ctx, add_parts
    ).astype(jnp.bfloat16)
    every_pos = recompute_pos[0]
    own_pos = lax.dynamic_slice_in_dim(every_pos, my_ctx * RCP, RCP)
    matches = jnp.arange(CTX_DEV, dtype=jnp.int32)[:, None] == own_pos[None, :]
    placed = jnp.dot(
        matches.astype(jnp.bfloat16), recomputed, preferred_element_type=jnp.float32
    ).astype(jnp.bfloat16)
    context = jnp.where(jnp.any(matches, axis=1)[:, None], placed, context)
    key_width = KVH * HD
    key_rows = context[:, :key_width].reshape(CTX_DEV, KVH, HD)
    value_rows = context[:, key_width:].reshape(CTX_DEV, KVH, HD)
    key_pos = my_ctx * CTX_DEV + jnp.arange(CTX_DEV, dtype=jnp.int32)
    key_in_use = key_pos // BLK < my_count
    mask_cols = block_mask[0]
    query_count = cycle_size * RCP
    query_pos = jnp.arange(query_count, dtype=jnp.int32) // RCP * CTX_DEV + every_pos
    all_queries = gather_rows(queries[0], my_ctx)
    per_group = QH // KVH
    allowed = jnp.take(mask_cols, query_pos // BLK, axis=0)
    visible = jnp.repeat(allowed, BLK, axis=1) > 0
    visible = visible & key_in_use[None, :] & (key_pos[None, :] <= query_pos[:, None])
    grouped = all_queries.reshape(query_count, KVH, per_group, HD)
    scores = jnp.einsum(
        "rkgd,tkd->kgrt", grouped, key_rows, preferred_element_type=jnp.float32
    ) * HD ** (-0.5)
    scores = jnp.where(visible[None, None], scores, -1e30)
    local_max = jnp.max(scores, axis=3)
    weights = jnp.where(visible[None, None], jnp.exp(scores - local_max[..., None]), 0.0)
    local_sum = jnp.sum(weights, axis=3)
    weighted = jnp.einsum(
        "kgrt,tkd->rkgd",
        weights.astype(jnp.bfloat16),
        value_rows,
        preferred_element_type=jnp.float32,
    )
    running = jnp.transpose(local_max, (2, 0, 1)).reshape(query_count, QH)
    totals = jnp.transpose(local_sum, (2, 0, 1)).reshape(query_count, QH)
    numerator = weighted.reshape(query_count, QH, HD)
    numerator, running, totals = scatter_rows(
        (
            numerator.reshape(cycle_size, RCP, QH, HD),
            running.reshape(cycle_size, RCP, QH),
            totals.reshape(cycle_size, RCP, QH),
        ),
        my_ctx,
        merge_softmax,
    )
    result = numerator / totals[:, :, None]
    attended = result.reshape(RCP, QH * HD).astype(jnp.bfloat16)
    return (context[None], attended[None])


def solution(mesh):
    in_specs = (
        P(("owner", "ctx"), None, None),
        P(None, "ctx"),
        P(),
        P("owner", None),
        P("owner", None, "ctx"),
        P("ctx", None),
        P("owner", "ctx", None),
        P("owner", None, "ctx"),
    )
    out_specs = (P("owner", "ctx", None), P("owner", "ctx", None))
    return jax.shard_map(
        on_device, mesh=mesh, in_specs=in_specs, out_specs=out_specs, check_vma=False
    )
```

```python
import jax
import jax.numpy as jnp
from jax import lax
from jax.experimental import pallas as pl
from jax.experimental.pallas import tpu as pltpu
from jax.sharding import PartitionSpec as P

QH = 32
KVH = 4
HD = 128
BLK = 128
NBD = 8
RCP = 8
SLOTS = 8
CAP = 4
CTX_DEV = 1024


def exchange(shard, bit):
    peers = lax.axis_size("ctx")
    return lax.ppermute(shard, "ctx", [(i, i ^ bit) for i in range(peers)])


def gather_rows(block, my_ctx):
    peers = lax.axis_size("ctx")
    held = block
    bit = 1
    while bit < peers:
        other = exchange(held, bit)
        upper = (my_ctx // bit) % 2 == 1
        held = jnp.where(
            upper, jnp.concatenate([other, held]), jnp.concatenate([held, other])
        )
        bit *= 2
    return held


def scatter_rows(parts, my_ctx, merge):
    peers = lax.axis_size("ctx")
    held = parts
    bit = 1
    while bit < peers:
        half = jax.tree.map(lambda a: a.reshape((a.shape[0] // 2, 2) + a.shape[1:]), held)
        upper = (my_ctx // bit) % 2 == 1
        keep = jax.tree.map(lambda a: jnp.where(upper, a[:, 1], a[:, 0]), half)
        send = jax.tree.map(lambda a: jnp.where(upper, a[:, 0], a[:, 1]), half)
        held = merge(keep, exchange(send, bit))
        bit *= 2
    return jax.tree.map(lambda a: a[0], held)


def add_parts(a, b):
    return a + b


def merge_softmax(a, b):
    numerator_a, running_a, totals_a = a
    numerator_b, running_b, totals_b = b
    newest = jnp.maximum(running_a, running_b)
    factor_a = jnp.exp(running_a - newest)
    factor_b = jnp.exp(running_b - newest)
    numerator = numerator_a * factor_a[..., None] + numerator_b * factor_b[..., None]
    return (numerator, newest, totals_a * factor_a + totals_b * factor_b)


def attend_kernel(query_ref, key_ref, value_ref, mask_ref, numerator_ref, running_ref, totals_ref):
    per_group = QH // KVH
    visible = mask_ref[...] > 0
    keys = key_ref[...]
    values = value_ref[...]
    for head in range(per_group):
        columns = slice(head * HD, (head + 1) * HD)
        scores = lax.dot_general(
            query_ref[:, columns],
            keys,
            (((1,), (1,)), ((), ())),
            preferred_element_type=jnp.float32,
        ) * HD ** (-0.5)
        scores = jnp.where(visible, scores, -1e30)
        highest = jnp.max(scores, axis=1, keepdims=True)
        weights = jnp.where(visible, jnp.exp(scores - highest), 0.0)
        numerator_ref[:, columns] = jnp.dot(
            weights.astype(jnp.bfloat16), values, preferred_element_type=jnp.float32
        )
        running_ref[0, :, head : head + 1] = highest
        totals_ref[0, :, head : head + 1] = jnp.sum(weights, axis=1, keepdims=True)


def attend_local(all_queries, key_rows, value_rows, visible):
    rows = all_queries.shape[0]
    keys = key_rows.shape[0]
    per_group = QH // KVH
    width = per_group * HD
    return pl.pallas_call(
        attend_kernel,
        grid=(KVH,),
        in_specs=[
            pl.BlockSpec((rows, width), lambda k: (0, k)),
            pl.BlockSpec((keys, HD), lambda k: (0, k)),
            pl.BlockSpec((keys, HD), lambda k: (0, k)),
            pl.BlockSpec((rows, keys), lambda k: (0, 0)),
        ],
        out_specs=[
            pl.BlockSpec((rows, width), lambda k: (0, k)),
            pl.BlockSpec((1, rows, per_group), lambda k: (k, 0, 0)),
            pl.BlockSpec((1, rows, per_group), lambda k: (k, 0, 0)),
        ],
        out_shape=[
            jax.ShapeDtypeStruct((rows, QH * HD), jnp.float32),
            jax.ShapeDtypeStruct((KVH, rows, per_group), jnp.float32),
            jax.ShapeDtypeStruct((KVH, rows, per_group), jnp.float32),
        ],
        cost_estimate=pl.CostEstimate(
            flops=4 * rows * keys * QH * HD,
            transcendentals=rows * keys * QH,
            bytes_accessed=rows * QH * HD * 6 + keys * KVH * HD * 4 + rows * keys * 4,
        ),
    )(all_queries, key_rows, value_rows, visible)

def on_device(span_cache, retrieval, counts, recompute_pos, hidden, kv_weight, queries, block_mask):
    owner_count = lax.axis_size("owner")
    cycle_size = lax.axis_size("ctx")
    my_owner = lax.axis_index("owner")
    my_ctx = lax.axis_index("ctx")
    feature_count = span_cache.shape[2]
    positions = jnp.arange(NBD, dtype=jnp.int32)
    block_ids = my_ctx * NBD + positions
    in_use = block_ids[None, :] < counts[:, None]
    holder = retrieval // (cycle_size * SLOTS)
    outbound = in_use & (holder == my_owner)
    slot_rank = jnp.cumsum(outbound.astype(jnp.int32), axis=1) - 1
    picked = outbound[:, None, :] & (
        slot_rank[:, None, :] == jnp.arange(CAP, dtype=jnp.int32)[None, :, None]
    )
    chosen = jnp.sum(jnp.where(picked, (retrieval % SLOTS)[:, None, :], 0), axis=2)
    filled = jnp.any(picked, axis=2)
    outgoing = jnp.where(
        filled[:, :, None, None], jnp.take(span_cache, chosen, axis=0), jnp.zeros((), jnp.bfloat16)
    )
    arrived = lax.all_to_all(outgoing, "owner", split_axis=0, concat_axis=0, tiled=True)
    wanted = lax.dynamic_index_in_dim(retrieval, my_owner, 0, keepdims=False)
    my_count = lax.dynamic_index_in_dim(counts, my_owner, 0, keepdims=False)
    my_in_use = block_ids < my_count
    source = wanted // (cycle_size * SLOTS)
    earlier = (
        (source[:, None] == source[None, :])
        & my_in_use[None, :]
        & (positions[None, :] < positions[:, None])
    )
    ordinal = jnp.sum(earlier.astype(jnp.int32), axis=1)
    flattened = arrived.reshape(owner_count * CAP, BLK, feature_count)
    blocks = jnp.take(flattened, source * CAP + ordinal, axis=0, mode="clip")
    blocks = jnp.where(my_in_use[:, None, None], blocks, jnp.zeros((), jnp.bfloat16))
    context = blocks.reshape(CTX_DEV, feature_count)
    local_rows = hidden[0]
    partial = jnp.dot(local_rows, kv_weight, preferred_element_type=jnp.float32)
    recomputed = scatter_rows(
        partial.reshape(cycle_size, RCP, feature_count), my_ctx, add_parts
    ).astype(jnp.bfloat16)
    every_pos = recompute_pos[0]
    own_pos = lax.dynamic_slice_in_dim(every_pos, my_ctx * RCP, RCP)
    matches = jnp.arange(CTX_DEV, dtype=jnp.int32)[:, None] == own_pos[None, :]
    placed = jnp.dot(
        matches.astype(jnp.bfloat16), recomputed, preferred_element_type=jnp.float32
    ).astype(jnp.bfloat16)
    context = jnp.where(jnp.any(matches, axis=1)[:, None], placed, context)
    key_width = KVH * HD
    key_pos = my_ctx * CTX_DEV + jnp.arange(CTX_DEV, dtype=jnp.int32)
    key_in_use = key_pos // BLK < my_count
    mask_cols = block_mask[0]
    query_count = cycle_size * RCP
    query_pos = jnp.arange(query_count, dtype=jnp.int32) // RCP * CTX_DEV + every_pos
    all_queries = gather_rows(queries[0], my_ctx)
    per_group = QH // KVH
    allowed = jnp.take(mask_cols, query_pos // BLK, axis=0)
    visible = jnp.repeat(allowed, BLK, axis=1) > 0
    visible = visible & key_in_use[None, :] & (key_pos[None, :] <= query_pos[:, None])
    numerator, running, totals = attend_local(
        all_queries,
        context[:, :key_width],
        context[:, key_width:],
        visible.astype(jnp.float32),
    )
    running = jnp.transpose(running, (1, 0, 2)).reshape(query_count, QH)
    totals = jnp.transpose(totals, (1, 0, 2)).reshape(query_count, QH)
    numerator = numerator.reshape(query_count, QH, HD)
    numerator, running, totals = scatter_rows(
        (
            numerator.reshape(cycle_size, RCP, QH, HD),
            running.reshape(cycle_size, RCP, QH),
            totals.reshape(cycle_size, RCP, QH),
        ),
        my_ctx,
        merge_softmax,
    )
    result = numerator / totals[:, :, None]
    attended = result.reshape(RCP, QH * HD).astype(jnp.bfloat16)
    return (context[None], attended[None])


def solution(mesh):
    in_specs = (
        P(("owner", "ctx"), None, None),
        P(None, "ctx"),
        P(),
        P("owner", None),
        P("owner", None, "ctx"),
        P("ctx", None),
        P("owner", "ctx", None),
        P("owner", None, "ctx"),
    )
    out_specs = (P("owner", "ctx", None), P("owner", "ctx", None))
    return jax.shard_map(
        on_device, mesh=mesh, in_specs=in_specs, out_specs=out_specs, check_vma=False
    )
```

```python
import jax
import jax.numpy as jnp
from jax import lax
from jax.experimental import pallas as pl
from jax.experimental.pallas import tpu as pltpu
from jax.sharding import PartitionSpec as P

QH = 32
KVH = 4
HD = 128
BLK = 128
NBD = 8
RCP = 8
SLOTS = 8
CAP = 4
CTX_DEV = 1024


def exchange(shard, bit):
    peers = lax.axis_size("ctx")
    return lax.ppermute(shard, "ctx", [(i, i ^ bit) for i in range(peers)])


def gather_rows(block, my_ctx):
    peers = lax.axis_size("ctx")
    held = block
    bit = 1
    while bit < peers:
        other = exchange(held, bit)
        upper = (my_ctx // bit) % 2 == 1
        held = jnp.where(
            upper, jnp.concatenate([other, held]), jnp.concatenate([held, other])
        )
        bit *= 2
    return held


def scatter_rows(parts, my_ctx, merge, narrow=lambda t: t, widen=lambda t: t):
    peers = lax.axis_size("ctx")
    held = parts
    bit = 1
    while bit < peers:
        half = jax.tree.map(lambda a: a.reshape((a.shape[0] // 2, 2) + a.shape[1:]), held)
        upper = (my_ctx // bit) % 2 == 1
        keep = jax.tree.map(lambda a: jnp.where(upper, a[:, 1], a[:, 0]), half)
        send = jax.tree.map(lambda a: jnp.where(upper, a[:, 0], a[:, 1]), half)
        held = merge(keep, widen(exchange(narrow(send), bit)))
        bit *= 2
    return jax.tree.map(lambda a: a[0], held)


def add_parts(a, b):
    return a + b


def merge_softmax(a, b):
    numerator_a, running_a, totals_a = a
    numerator_b, running_b, totals_b = b
    newest = jnp.maximum(running_a, running_b)
    factor_a = jnp.exp(running_a - newest)
    factor_b = jnp.exp(running_b - newest)
    numerator = numerator_a * factor_a[..., None] + numerator_b * factor_b[..., None]
    return (numerator, newest, totals_a * factor_a + totals_b * factor_b)


def attend_kernel(query_ref, key_ref, value_ref, mask_ref, numerator_ref, running_ref, totals_ref):
    per_group = QH // KVH
    visible = mask_ref[...] > 0
    keys = key_ref[...]
    values = value_ref[...]
    for head in range(per_group):
        columns = slice(head * HD, (head + 1) * HD)
        scores = lax.dot_general(
            query_ref[:, columns],
            keys,
            (((1,), (1,)), ((), ())),
            preferred_element_type=jnp.float32,
        ) * HD ** (-0.5)
        scores = jnp.where(visible, scores, -1e30)
        highest = jnp.max(scores, axis=1, keepdims=True)
        weights = jnp.where(visible, jnp.exp(scores - highest), 0.0)
        numerator_ref[:, columns] = jnp.dot(
            weights.astype(jnp.bfloat16), values, preferred_element_type=jnp.float32
        )
        running_ref[0, :, head : head + 1] = highest
        totals_ref[0, :, head : head + 1] = jnp.sum(weights, axis=1, keepdims=True)


def attend_local(all_queries, key_rows, value_rows, visible):
    rows = all_queries.shape[0]
    keys = key_rows.shape[0]
    per_group = QH // KVH
    width = per_group * HD
    return pl.pallas_call(
        attend_kernel,
        grid=(KVH,),
        in_specs=[
            pl.BlockSpec((rows, width), lambda k: (0, k)),
            pl.BlockSpec((keys, HD), lambda k: (0, k)),
            pl.BlockSpec((keys, HD), lambda k: (0, k)),
            pl.BlockSpec((rows, keys), lambda k: (0, 0)),
        ],
        out_specs=[
            pl.BlockSpec((rows, width), lambda k: (0, k)),
            pl.BlockSpec((1, rows, per_group), lambda k: (k, 0, 0)),
            pl.BlockSpec((1, rows, per_group), lambda k: (k, 0, 0)),
        ],
        out_shape=[
            jax.ShapeDtypeStruct((rows, QH * HD), jnp.float32),
            jax.ShapeDtypeStruct((KVH, rows, per_group), jnp.float32),
            jax.ShapeDtypeStruct((KVH, rows, per_group), jnp.float32),
        ],
        cost_estimate=pl.CostEstimate(
            flops=4 * rows * keys * QH * HD,
            transcendentals=rows * keys * QH,
            bytes_accessed=rows * QH * HD * 6 + keys * KVH * HD * 4 + rows * keys * 4,
        ),
    )(all_queries, key_rows, value_rows, visible)

def on_device(span_cache, retrieval, counts, recompute_pos, hidden, kv_weight, queries, block_mask):
    owner_count = lax.axis_size("owner")
    cycle_size = lax.axis_size("ctx")
    my_owner = lax.axis_index("owner")
    my_ctx = lax.axis_index("ctx")
    feature_count = span_cache.shape[2]
    positions = jnp.arange(NBD, dtype=jnp.int32)
    block_ids = my_ctx * NBD + positions
    in_use = block_ids[None, :] < counts[:, None]
    holder = retrieval // (cycle_size * SLOTS)
    outbound = in_use & (holder == my_owner)
    slot_rank = jnp.cumsum(outbound.astype(jnp.int32), axis=1) - 1
    picked = outbound[:, None, :] & (
        slot_rank[:, None, :] == jnp.arange(CAP, dtype=jnp.int32)[None, :, None]
    )
    chosen = jnp.sum(jnp.where(picked, (retrieval % SLOTS)[:, None, :], 0), axis=2)
    filled = jnp.any(picked, axis=2)
    outgoing = jnp.where(
        filled[:, :, None, None], jnp.take(span_cache, chosen, axis=0), jnp.zeros((), jnp.bfloat16)
    )
    arrived = lax.all_to_all(outgoing, "owner", split_axis=0, concat_axis=0, tiled=True)
    wanted = lax.dynamic_index_in_dim(retrieval, my_owner, 0, keepdims=False)
    my_count = lax.dynamic_index_in_dim(counts, my_owner, 0, keepdims=False)
    my_in_use = block_ids < my_count
    source = wanted // (cycle_size * SLOTS)
    earlier = (
        (source[:, None] == source[None, :])
        & my_in_use[None, :]
        & (positions[None, :] < positions[:, None])
    )
    ordinal = jnp.sum(earlier.astype(jnp.int32), axis=1)
    flattened = arrived.reshape(owner_count * CAP, BLK, feature_count)
    blocks = jnp.take(flattened, source * CAP + ordinal, axis=0, mode="clip")
    blocks = jnp.where(my_in_use[:, None, None], blocks, jnp.zeros((), jnp.bfloat16))
    context = blocks.reshape(CTX_DEV, feature_count)
    local_rows = hidden[0]
    partial = jnp.dot(local_rows, kv_weight, preferred_element_type=jnp.float32)
    recomputed = scatter_rows(
        partial.reshape(cycle_size, RCP, feature_count), my_ctx, add_parts
    ).astype(jnp.bfloat16)
    every_pos = recompute_pos[0]
    own_pos = lax.dynamic_slice_in_dim(every_pos, my_ctx * RCP, RCP)
    matches = jnp.arange(CTX_DEV, dtype=jnp.int32)[:, None] == own_pos[None, :]
    placed = jnp.dot(
        matches.astype(jnp.bfloat16), recomputed, preferred_element_type=jnp.float32
    ).astype(jnp.bfloat16)
    context = jnp.where(jnp.any(matches, axis=1)[:, None], placed, context)
    key_width = KVH * HD
    key_pos = my_ctx * CTX_DEV + jnp.arange(CTX_DEV, dtype=jnp.int32)
    key_in_use = key_pos // BLK < my_count
    mask_cols = block_mask[0]
    query_count = cycle_size * RCP
    query_pos = jnp.arange(query_count, dtype=jnp.int32) // RCP * CTX_DEV + every_pos
    all_queries = gather_rows(queries[0], my_ctx)
    per_group = QH // KVH
    allowed = jnp.take(mask_cols, query_pos // BLK, axis=0)
    visible = jnp.repeat(allowed, BLK, axis=1) > 0
    visible = visible & key_in_use[None, :] & (key_pos[None, :] <= query_pos[:, None])
    numerator, running, totals = attend_local(
        all_queries,
        context[:, :key_width],
        context[:, key_width:],
        visible.astype(jnp.float32),
    )
    running = jnp.transpose(running, (1, 0, 2)).reshape(query_count, QH)
    totals = jnp.transpose(totals, (1, 0, 2)).reshape(query_count, QH)
    numerator = numerator.reshape(query_count, QH, HD)
    numerator, running, totals = scatter_rows(
        (
            numerator.reshape(cycle_size, RCP, QH, HD),
            running.reshape(cycle_size, RCP, QH),
            totals.reshape(cycle_size, RCP, QH),
        ),
        my_ctx,
        merge_softmax,
        lambda t: (t[0].astype(jnp.bfloat16),) + t[1:],
        lambda t: (t[0].astype(jnp.float32),) + t[1:],
    )
    result = numerator / totals[:, :, None]
    attended = result.reshape(RCP, QH * HD).astype(jnp.bfloat16)
    return (context[None], attended[None])


def solution(mesh):
    in_specs = (
        P(("owner", "ctx"), None, None),
        P(None, "ctx"),
        P(),
        P("owner", None),
        P("owner", None, "ctx"),
        P("ctx", None),
        P("owner", "ctx", None),
        P("owner", None, "ctx"),
    )
    out_specs = (P("owner", "ctx", None), P("owner", "ctx", None))
    return jax.shard_map(
        on_device, mesh=mesh, in_specs=in_specs, out_specs=out_specs, check_vma=False
    )
```

```python
import jax
import jax.numpy as jnp
from jax import lax
from jax.experimental import pallas as pl
from jax.experimental.pallas import tpu as pltpu
from jax.sharding import PartitionSpec as P

QH = 32
KVH = 4
HD = 128
BLK = 128
NBD = 8
RCP = 8
SLOTS = 8
CAP = 4
CTX_DEV = 1024


def exchange(shard, bit):
    peers = lax.axis_size("ctx")
    return lax.ppermute(shard, "ctx", [(i, i ^ bit) for i in range(peers)])


def gather_rows(block, my_ctx):
    peers = lax.axis_size("ctx")
    held = block
    bit = 1
    while bit < peers:
        other = exchange(held, bit)
        upper = (my_ctx // bit) % 2 == 1
        held = jnp.where(
            upper, jnp.concatenate([other, held]), jnp.concatenate([held, other])
        )
        bit *= 2
    return held


def scatter_rows(parts, my_ctx, merge, narrow=lambda t: t, widen=lambda t: t):
    peers = lax.axis_size("ctx")
    held = parts
    bit = 1
    while bit < peers:
        half = jax.tree.map(lambda a: a.reshape((a.shape[0] // 2, 2) + a.shape[1:]), held)
        upper = (my_ctx // bit) % 2 == 1
        keep = jax.tree.map(lambda a: jnp.where(upper, a[:, 1], a[:, 0]), half)
        send = jax.tree.map(lambda a: jnp.where(upper, a[:, 0], a[:, 1]), half)
        held = merge(keep, widen(exchange(narrow(send), bit)))
        bit *= 2
    return jax.tree.map(lambda a: a[0], held)


def add_parts(a, b):
    return a + b


def merge_softmax(a, b):
    numerator_a, running_a, totals_a = a
    numerator_b, running_b, totals_b = b
    newest = jnp.maximum(running_a, running_b)
    factor_a = jnp.exp(running_a - newest)
    factor_b = jnp.exp(running_b - newest)
    numerator = numerator_a * factor_a[..., None] + numerator_b * factor_b[..., None]
    return (numerator, newest, totals_a * factor_a + totals_b * factor_b)


def attend_kernel(query_ref, key_ref, value_ref, mask_ref, numerator_ref, running_ref, totals_ref):
    per_group = QH // KVH
    visible = mask_ref[...] > 0
    keys = key_ref[...]
    values = value_ref[...]
    for head in range(per_group):
        columns = slice(head * HD, (head + 1) * HD)
        scores = lax.dot_general(
            query_ref[:, columns],
            keys,
            (((1,), (1,)), ((), ())),
            preferred_element_type=jnp.float32,
        ) * HD ** (-0.5)
        scores = jnp.where(visible, scores, -1e30)
        highest = jnp.max(scores, axis=1, keepdims=True)
        weights = jnp.where(visible, jnp.exp(scores - highest), 0.0)
        numerator_ref[:, columns] = jnp.dot(
            weights.astype(jnp.bfloat16), values, preferred_element_type=jnp.float32
        )
        running_ref[0, :, head : head + 1] = highest
        totals_ref[0, :, head : head + 1] = jnp.sum(weights, axis=1, keepdims=True)


def attend_local(all_queries, key_rows, value_rows, visible):
    rows = all_queries.shape[0]
    keys = key_rows.shape[0]
    per_group = QH // KVH
    width = per_group * HD
    return pl.pallas_call(
        attend_kernel,
        grid=(KVH,),
        in_specs=[
            pl.BlockSpec((rows, width), lambda k: (0, k)),
            pl.BlockSpec((keys, HD), lambda k: (0, k)),
            pl.BlockSpec((keys, HD), lambda k: (0, k)),
            pl.BlockSpec((rows, keys), lambda k: (0, 0)),
        ],
        out_specs=[
            pl.BlockSpec((rows, width), lambda k: (0, k)),
            pl.BlockSpec((1, rows, per_group), lambda k: (k, 0, 0)),
            pl.BlockSpec((1, rows, per_group), lambda k: (k, 0, 0)),
        ],
        out_shape=[
            jax.ShapeDtypeStruct((rows, QH * HD), jnp.float32),
            jax.ShapeDtypeStruct((KVH, rows, per_group), jnp.float32),
            jax.ShapeDtypeStruct((KVH, rows, per_group), jnp.float32),
        ],
        cost_estimate=pl.CostEstimate(
            flops=4 * rows * keys * QH * HD,
            transcendentals=rows * keys * QH,
            bytes_accessed=rows * QH * HD * 6 + keys * KVH * HD * 4 + rows * keys * 4,
        ),
    )(all_queries, key_rows, value_rows, visible)

def on_device(span_cache, retrieval, counts, recompute_pos, hidden, kv_weight, queries, block_mask):
    owner_count = lax.axis_size("owner")
    cycle_size = lax.axis_size("ctx")
    my_owner = lax.axis_index("owner")
    my_ctx = lax.axis_index("ctx")
    feature_count = span_cache.shape[2]
    positions = jnp.arange(NBD, dtype=jnp.int32)
    block_ids = my_ctx * NBD + positions
    in_use = block_ids[None, :] < counts[:, None]
    holder = retrieval // (cycle_size * SLOTS)
    outbound = in_use & (holder == my_owner)
    slot_rank = jnp.cumsum(outbound.astype(jnp.int32), axis=1) - 1
    picked = outbound[:, None, :] & (
        slot_rank[:, None, :] == jnp.arange(CAP, dtype=jnp.int32)[None, :, None]
    )
    chosen = jnp.sum(jnp.where(picked, (retrieval % SLOTS)[:, None, :], 0), axis=2)
    filled = jnp.any(picked, axis=2)
    outgoing = jnp.where(
        filled[:, :, None, None], jnp.take(span_cache, chosen, axis=0), jnp.zeros((), jnp.bfloat16)
    )
    local_rows = hidden[0]
    partial = jnp.dot(local_rows, kv_weight, preferred_element_type=jnp.float32)
    recomputed = scatter_rows(
        partial.reshape(cycle_size, RCP, feature_count), my_ctx, add_parts
    ).astype(jnp.bfloat16)
    all_queries = gather_rows(queries[0], my_ctx)
    outgoing, recomputed, all_queries = lax.optimization_barrier(
        (outgoing, recomputed, all_queries)
    )
    arrived = lax.all_to_all(outgoing, "owner", split_axis=0, concat_axis=0, tiled=True)
    wanted = lax.dynamic_index_in_dim(retrieval, my_owner, 0, keepdims=False)
    my_count = lax.dynamic_index_in_dim(counts, my_owner, 0, keepdims=False)
    my_in_use = block_ids < my_count
    source = wanted // (cycle_size * SLOTS)
    earlier = (
        (source[:, None] == source[None, :])
        & my_in_use[None, :]
        & (positions[None, :] < positions[:, None])
    )
    ordinal = jnp.sum(earlier.astype(jnp.int32), axis=1)
    flattened = arrived.reshape(owner_count * CAP, BLK, feature_count)
    blocks = jnp.take(flattened, source * CAP + ordinal, axis=0, mode="clip")
    blocks = jnp.where(my_in_use[:, None, None], blocks, jnp.zeros((), jnp.bfloat16))
    context = blocks.reshape(CTX_DEV, feature_count)
    every_pos = recompute_pos[0]
    own_pos = lax.dynamic_slice_in_dim(every_pos, my_ctx * RCP, RCP)
    matches = jnp.arange(CTX_DEV, dtype=jnp.int32)[:, None] == own_pos[None, :]
    placed = jnp.dot(
        matches.astype(jnp.bfloat16), recomputed, preferred_element_type=jnp.float32
    ).astype(jnp.bfloat16)
    context = jnp.where(jnp.any(matches, axis=1)[:, None], placed, context)
    key_width = KVH * HD
    key_pos = my_ctx * CTX_DEV + jnp.arange(CTX_DEV, dtype=jnp.int32)
    key_in_use = key_pos // BLK < my_count
    mask_cols = block_mask[0]
    query_count = cycle_size * RCP
    query_pos = jnp.arange(query_count, dtype=jnp.int32) // RCP * CTX_DEV + every_pos
    per_group = QH // KVH
    allowed = jnp.take(mask_cols, query_pos // BLK, axis=0)
    visible = jnp.repeat(allowed, BLK, axis=1) > 0
    visible = visible & key_in_use[None, :] & (key_pos[None, :] <= query_pos[:, None])
    numerator, running, totals = attend_local(
        all_queries,
        context[:, :key_width],
        context[:, key_width:],
        visible.astype(jnp.float32),
    )
    running = jnp.transpose(running, (1, 0, 2)).reshape(query_count, QH)
    totals = jnp.transpose(totals, (1, 0, 2)).reshape(query_count, QH)
    numerator = numerator.reshape(query_count, QH, HD)
    numerator, running, totals = scatter_rows(
        (
            numerator.reshape(cycle_size, RCP, QH, HD),
            running.reshape(cycle_size, RCP, QH),
            totals.reshape(cycle_size, RCP, QH),
        ),
        my_ctx,
        merge_softmax,
        lambda t: (t[0].astype(jnp.bfloat16),) + t[1:],
        lambda t: (t[0].astype(jnp.float32),) + t[1:],
    )
    result = numerator / totals[:, :, None]
    attended = result.reshape(RCP, QH * HD).astype(jnp.bfloat16)
    return (context[None], attended[None])


def solution(mesh):
    in_specs = (
        P(("owner", "ctx"), None, None),
        P(None, "ctx"),
        P(),
        P("owner", None),
        P("owner", None, "ctx"),
        P("ctx", None),
        P("owner", "ctx", None),
        P("owner", None, "ctx"),
    )
    out_specs = (P("owner", "ctx", None), P("owner", "ctx", None))
    return jax.shard_map(
        on_device, mesh=mesh, in_specs=in_specs, out_specs=out_specs, check_vma=False
    )
```

```python
import jax
import jax.numpy as jnp
from jax import lax
from jax.experimental import pallas as pl
from jax.experimental.pallas import tpu as pltpu
from jax.sharding import PartitionSpec as P

QH = 32
KVH = 4
HD = 128
BLK = 128
NBD = 8
RCP = 8
SLOTS = 8
CAP = 4
CTX_DEV = 1024


def exchange(shard, bit):
    peers = lax.axis_size("ctx")
    return lax.ppermute(shard, "ctx", [(i, i ^ bit) for i in range(peers)])


def gather_rows(block, my_ctx):
    peers = lax.axis_size("ctx")
    held = block
    bit = 1
    while bit < peers:
        other = exchange(held, bit)
        upper = (my_ctx // bit) % 2 == 1
        held = jnp.where(
            upper, jnp.concatenate([other, held]), jnp.concatenate([held, other])
        )
        bit *= 2
    return held


def scatter_rows(parts, my_ctx, merge, narrow=lambda t: t, widen=lambda t: t):
    peers = lax.axis_size("ctx")
    held = parts
    bit = 1
    while bit < peers:
        half = jax.tree.map(lambda a: a.reshape((a.shape[0] // 2, 2) + a.shape[1:]), held)
        upper = (my_ctx // bit) % 2 == 1
        keep = jax.tree.map(lambda a: jnp.where(upper, a[:, 1], a[:, 0]), half)
        send = jax.tree.map(lambda a: jnp.where(upper, a[:, 0], a[:, 1]), half)
        held = merge(keep, widen(exchange(narrow(send), bit)))
        bit *= 2
    return jax.tree.map(lambda a: a[0], held)


def add_parts(a, b):
    return a + b


def merge_softmax(a, b):
    numerator_a, stats_a = a
    numerator_b, stats_b = b
    running_a, totals_a = stats_a[..., :QH], stats_a[..., QH:]
    running_b, totals_b = stats_b[..., :QH], stats_b[..., QH:]
    newest = jnp.maximum(running_a, running_b)
    factor_a = jnp.exp(running_a - newest)
    factor_b = jnp.exp(running_b - newest)
    numerator = numerator_a * factor_a[..., None] + numerator_b * factor_b[..., None]
    totals = totals_a * factor_a + totals_b * factor_b
    return (numerator, jnp.concatenate([newest, totals], axis=-1))


def attend_kernel(query_ref, key_ref, value_ref, mask_ref, numerator_ref, running_ref, totals_ref):
    per_group = QH // KVH
    visible = mask_ref[...] > 0
    keys = key_ref[...]
    values = value_ref[...]
    for head in range(per_group):
        columns = slice(head * HD, (head + 1) * HD)
        scores = lax.dot_general(
            query_ref[:, columns],
            keys,
            (((1,), (1,)), ((), ())),
            preferred_element_type=jnp.float32,
        ) * HD ** (-0.5)
        scores = jnp.where(visible, scores, -1e30)
        highest = jnp.max(scores, axis=1, keepdims=True)
        weights = jnp.where(visible, jnp.exp(scores - highest), 0.0)
        numerator_ref[:, columns] = jnp.dot(
            weights.astype(jnp.bfloat16), values, preferred_element_type=jnp.float32
        )
        running_ref[0, :, head : head + 1] = highest
        totals_ref[0, :, head : head + 1] = jnp.sum(weights, axis=1, keepdims=True)


def attend_local(all_queries, key_rows, value_rows, visible):
    rows = all_queries.shape[0]
    keys = key_rows.shape[0]
    per_group = QH // KVH
    width = per_group * HD
    return pl.pallas_call(
        attend_kernel,
        grid=(KVH,),
        in_specs=[
            pl.BlockSpec((rows, width), lambda k: (0, k)),
            pl.BlockSpec((keys, HD), lambda k: (0, k)),
            pl.BlockSpec((keys, HD), lambda k: (0, k)),
            pl.BlockSpec((rows, keys), lambda k: (0, 0)),
        ],
        out_specs=[
            pl.BlockSpec((rows, width), lambda k: (0, k)),
            pl.BlockSpec((1, rows, per_group), lambda k: (k, 0, 0)),
            pl.BlockSpec((1, rows, per_group), lambda k: (k, 0, 0)),
        ],
        out_shape=[
            jax.ShapeDtypeStruct((rows, QH * HD), jnp.float32),
            jax.ShapeDtypeStruct((KVH, rows, per_group), jnp.float32),
            jax.ShapeDtypeStruct((KVH, rows, per_group), jnp.float32),
        ],
        cost_estimate=pl.CostEstimate(
            flops=4 * rows * keys * QH * HD,
            transcendentals=rows * keys * QH,
            bytes_accessed=rows * QH * HD * 6 + keys * KVH * HD * 4 + rows * keys * 4,
        ),
    )(all_queries, key_rows, value_rows, visible)

def on_device(span_cache, retrieval, counts, recompute_pos, hidden, kv_weight, queries, block_mask):
    owner_count = lax.axis_size("owner")
    cycle_size = lax.axis_size("ctx")
    my_owner = lax.axis_index("owner")
    my_ctx = lax.axis_index("ctx")
    feature_count = span_cache.shape[2]
    positions = jnp.arange(NBD, dtype=jnp.int32)
    block_ids = my_ctx * NBD + positions
    in_use = block_ids[None, :] < counts[:, None]
    holder = retrieval // (cycle_size * SLOTS)
    outbound = in_use & (holder == my_owner)
    slot_rank = jnp.cumsum(outbound.astype(jnp.int32), axis=1) - 1
    picked = outbound[:, None, :] & (
        slot_rank[:, None, :] == jnp.arange(CAP, dtype=jnp.int32)[None, :, None]
    )
    chosen = jnp.sum(jnp.where(picked, (retrieval % SLOTS)[:, None, :], 0), axis=2)
    filled = jnp.any(picked, axis=2)
    outgoing = jnp.where(
        filled[:, :, None, None], jnp.take(span_cache, chosen, axis=0), jnp.zeros((), jnp.bfloat16)
    )
    local_rows = hidden[0]
    partial = jnp.dot(local_rows, kv_weight, preferred_element_type=jnp.float32)
    recomputed = scatter_rows(
        partial.reshape(cycle_size, RCP, feature_count), my_ctx, add_parts
    ).astype(jnp.bfloat16)
    all_queries = gather_rows(queries[0], my_ctx)
    outgoing, recomputed, all_queries = lax.optimization_barrier(
        (outgoing, recomputed, all_queries)
    )
    arrived = lax.all_to_all(outgoing, "owner", split_axis=0, concat_axis=0, tiled=True)
    wanted = lax.dynamic_index_in_dim(retrieval, my_owner, 0, keepdims=False)
    my_count = lax.dynamic_index_in_dim(counts, my_owner, 0, keepdims=False)
    my_in_use = block_ids < my_count
    source = wanted // (cycle_size * SLOTS)
    earlier = (
        (source[:, None] == source[None, :])
        & my_in_use[None, :]
        & (positions[None, :] < positions[:, None])
    )
    ordinal = jnp.sum(earlier.astype(jnp.int32), axis=1)
    flattened = arrived.reshape(owner_count * CAP, BLK, feature_count)
    blocks = jnp.take(flattened, source * CAP + ordinal, axis=0, mode="clip")
    blocks = jnp.where(my_in_use[:, None, None], blocks, jnp.zeros((), jnp.bfloat16))
    context = blocks.reshape(CTX_DEV, feature_count)
    every_pos = recompute_pos[0]
    own_pos = lax.dynamic_slice_in_dim(every_pos, my_ctx * RCP, RCP)
    matches = jnp.arange(CTX_DEV, dtype=jnp.int32)[:, None] == own_pos[None, :]
    placed = jnp.dot(
        matches.astype(jnp.bfloat16), recomputed, preferred_element_type=jnp.float32
    ).astype(jnp.bfloat16)
    context = jnp.where(jnp.any(matches, axis=1)[:, None], placed, context)
    key_width = KVH * HD
    key_pos = my_ctx * CTX_DEV + jnp.arange(CTX_DEV, dtype=jnp.int32)
    key_in_use = key_pos // BLK < my_count
    mask_cols = block_mask[0]
    query_count = cycle_size * RCP
    query_pos = jnp.arange(query_count, dtype=jnp.int32) // RCP * CTX_DEV + every_pos
    per_group = QH // KVH
    allowed = jnp.take(mask_cols, query_pos // BLK, axis=0)
    visible = jnp.repeat(allowed, BLK, axis=1) > 0
    visible = visible & key_in_use[None, :] & (key_pos[None, :] <= query_pos[:, None])
    numerator, running, totals = attend_local(
        all_queries,
        context[:, :key_width],
        context[:, key_width:],
        visible.astype(jnp.float32),
    )
    running = jnp.transpose(running, (1, 0, 2)).reshape(query_count, QH)
    totals = jnp.transpose(totals, (1, 0, 2)).reshape(query_count, QH)
    numerator = numerator.reshape(query_count, QH, HD)
    numerator, stats = scatter_rows(
        (
            numerator.reshape(cycle_size, RCP, QH, HD),
            jnp.concatenate([running, totals], axis=-1).reshape(cycle_size, RCP, 2 * QH),
        ),
        my_ctx,
        merge_softmax,
        lambda t: (t[0].astype(jnp.bfloat16), t[1]),
        lambda t: (t[0].astype(jnp.float32), t[1]),
    )
    totals = stats[:, QH:]
    result = numerator / totals[:, :, None]
    attended = result.reshape(RCP, QH * HD).astype(jnp.bfloat16)
    return (context[None], attended[None])


def solution(mesh):
    in_specs = (
        P(("owner", "ctx"), None, None),
        P(None, "ctx"),
        P(),
        P("owner", None),
        P("owner", None, "ctx"),
        P("ctx", None),
        P("owner", "ctx", None),
        P("owner", None, "ctx"),
    )
    out_specs = (P("owner", "ctx", None), P("owner", "ctx", None))
    return jax.shard_map(
        on_device, mesh=mesh, in_specs=in_specs, out_specs=out_specs, check_vma=False
    )
```

```python
import jax
import jax.numpy as jnp
from jax import lax
from jax.experimental import pallas as pl
from jax.experimental.pallas import tpu as pltpu
from jax.sharding import PartitionSpec as P

QH = 32
KVH = 4
HD = 128
BLK = 128
NBD = 8
RCP = 8
SLOTS = 8
CAP = 4
CTX_DEV = 1024


def digit_plan(peers):
    plan = []
    stride = 1
    while stride < peers:
        radix = 4 if peers // stride >= 4 else 2
        plan.append((stride, radix))
        stride *= radix
    return plan


def shifted(shard, stride, radix, step):
    peers = lax.axis_size("ctx")
    pairs = []
    for i in range(peers):
        digit = (i // stride) % radix
        pairs.append((i, i + ((digit + step) % radix - digit) * stride))
    return lax.ppermute(shard, "ctx", pairs)


def gather_rows(block, my_ctx):
    held = block
    for stride, radix in digit_plan(lax.axis_size("ctx")):
        digit = (my_ctx // stride) % radix
        pieces = [held] + [shifted(held, stride, radix, step) for step in range(1, radix)]
        order = (digit - jnp.arange(radix, dtype=jnp.int32)) % radix
        held = jnp.take(jnp.stack(pieces), order, axis=0)
        held = held.reshape((radix * block.shape[0] * stride,) + block.shape[1:])
    return held


def scatter_rows(parts, my_ctx, merge, narrow=lambda t: t, widen=lambda t: t):
    held = parts
    for stride, radix in digit_plan(lax.axis_size("ctx")):
        digit = (my_ctx // stride) % radix
        grouped = jax.tree.map(
            lambda a: a.reshape((a.shape[0] // radix, radix) + a.shape[1:]), held
        )
        merged = jax.tree.map(lambda a: jnp.take(a, digit, axis=1), grouped)
        for step in range(1, radix):
            target = (digit + step) % radix
            send = jax.tree.map(lambda a: jnp.take(a, target, axis=1), grouped)
            merged = merge(merged, widen(shifted(narrow(send), stride, radix, step)))
        held = merged
    return jax.tree.map(lambda a: a[0], held)


def add_parts(a, b):
    return a + b


def merge_softmax(a, b):
    numerator_a, stats_a = a
    numerator_b, stats_b = b
    running_a, totals_a = stats_a[..., :QH], stats_a[..., QH:]
    running_b, totals_b = stats_b[..., :QH], stats_b[..., QH:]
    newest = jnp.maximum(running_a, running_b)
    factor_a = jnp.exp(running_a - newest)
    factor_b = jnp.exp(running_b - newest)
    numerator = numerator_a * factor_a[..., None] + numerator_b * factor_b[..., None]
    totals = totals_a * factor_a + totals_b * factor_b
    return (numerator, jnp.concatenate([newest, totals], axis=-1))


def attend_kernel(query_ref, key_ref, value_ref, mask_ref, numerator_ref, running_ref, totals_ref):
    per_group = QH // KVH
    visible = mask_ref[...] > 0
    keys = key_ref[...]
    values = value_ref[...]
    for head in range(per_group):
        columns = slice(head * HD, (head + 1) * HD)
        scores = lax.dot_general(
            query_ref[:, columns],
            keys,
            (((1,), (1,)), ((), ())),
            preferred_element_type=jnp.float32,
        ) * HD ** (-0.5)
        scores = jnp.where(visible, scores, -1e30)
        highest = jnp.max(scores, axis=1, keepdims=True)
        weights = jnp.where(visible, jnp.exp(scores - highest), 0.0)
        numerator_ref[:, columns] = jnp.dot(
            weights.astype(jnp.bfloat16), values, preferred_element_type=jnp.float32
        )
        running_ref[0, :, head : head + 1] = highest
        totals_ref[0, :, head : head + 1] = jnp.sum(weights, axis=1, keepdims=True)


def attend_local(all_queries, key_rows, value_rows, visible):
    rows = all_queries.shape[0]
    keys = key_rows.shape[0]
    per_group = QH // KVH
    width = per_group * HD
    return pl.pallas_call(
        attend_kernel,
        grid=(KVH,),
        in_specs=[
            pl.BlockSpec((rows, width), lambda k: (0, k)),
            pl.BlockSpec((keys, HD), lambda k: (0, k)),
            pl.BlockSpec((keys, HD), lambda k: (0, k)),
            pl.BlockSpec((rows, keys), lambda k: (0, 0)),
        ],
        out_specs=[
            pl.BlockSpec((rows, width), lambda k: (0, k)),
            pl.BlockSpec((1, rows, per_group), lambda k: (k, 0, 0)),
            pl.BlockSpec((1, rows, per_group), lambda k: (k, 0, 0)),
        ],
        out_shape=[
            jax.ShapeDtypeStruct((rows, QH * HD), jnp.float32),
            jax.ShapeDtypeStruct((KVH, rows, per_group), jnp.float32),
            jax.ShapeDtypeStruct((KVH, rows, per_group), jnp.float32),
        ],
        cost_estimate=pl.CostEstimate(
            flops=4 * rows * keys * QH * HD,
            transcendentals=rows * keys * QH,
            bytes_accessed=rows * QH * HD * 6 + keys * KVH * HD * 4 + rows * keys * 4,
        ),
    )(all_queries, key_rows, value_rows, visible)

def on_device(span_cache, retrieval, counts, recompute_pos, hidden, kv_weight, queries, block_mask):
    owner_count = lax.axis_size("owner")
    cycle_size = lax.axis_size("ctx")
    my_owner = lax.axis_index("owner")
    my_ctx = lax.axis_index("ctx")
    feature_count = span_cache.shape[2]
    positions = jnp.arange(NBD, dtype=jnp.int32)
    block_ids = my_ctx * NBD + positions
    in_use = block_ids[None, :] < counts[:, None]
    holder = retrieval // (cycle_size * SLOTS)
    outbound = in_use & (holder == my_owner)
    slot_rank = jnp.cumsum(outbound.astype(jnp.int32), axis=1) - 1
    picked = outbound[:, None, :] & (
        slot_rank[:, None, :] == jnp.arange(CAP, dtype=jnp.int32)[None, :, None]
    )
    chosen = jnp.sum(jnp.where(picked, (retrieval % SLOTS)[:, None, :], 0), axis=2)
    filled = jnp.any(picked, axis=2)
    outgoing = jnp.where(
        filled[:, :, None, None], jnp.take(span_cache, chosen, axis=0), jnp.zeros((), jnp.bfloat16)
    )
    local_rows = hidden[0]
    partial = jnp.dot(local_rows, kv_weight, preferred_element_type=jnp.float32)
    recomputed = scatter_rows(
        partial.reshape(cycle_size, RCP, feature_count), my_ctx, add_parts
    ).astype(jnp.bfloat16)
    all_queries = gather_rows(queries[0], my_ctx)
    outgoing, recomputed, all_queries = lax.optimization_barrier(
        (outgoing, recomputed, all_queries)
    )
    arrived = lax.all_to_all(outgoing, "owner", split_axis=0, concat_axis=0, tiled=True)
    wanted = lax.dynamic_index_in_dim(retrieval, my_owner, 0, keepdims=False)
    my_count = lax.dynamic_index_in_dim(counts, my_owner, 0, keepdims=False)
    my_in_use = block_ids < my_count
    source = wanted // (cycle_size * SLOTS)
    earlier = (
        (source[:, None] == source[None, :])
        & my_in_use[None, :]
        & (positions[None, :] < positions[:, None])
    )
    ordinal = jnp.sum(earlier.astype(jnp.int32), axis=1)
    flattened = arrived.reshape(owner_count * CAP, BLK, feature_count)
    blocks = jnp.take(flattened, source * CAP + ordinal, axis=0, mode="clip")
    blocks = jnp.where(my_in_use[:, None, None], blocks, jnp.zeros((), jnp.bfloat16))
    context = blocks.reshape(CTX_DEV, feature_count)
    every_pos = recompute_pos[0]
    own_pos = lax.dynamic_slice_in_dim(every_pos, my_ctx * RCP, RCP)
    matches = jnp.arange(CTX_DEV, dtype=jnp.int32)[:, None] == own_pos[None, :]
    placed = jnp.dot(
        matches.astype(jnp.bfloat16), recomputed, preferred_element_type=jnp.float32
    ).astype(jnp.bfloat16)
    context = jnp.where(jnp.any(matches, axis=1)[:, None], placed, context)
    key_width = KVH * HD
    key_pos = my_ctx * CTX_DEV + jnp.arange(CTX_DEV, dtype=jnp.int32)
    key_in_use = key_pos // BLK < my_count
    mask_cols = block_mask[0]
    query_count = cycle_size * RCP
    query_pos = jnp.arange(query_count, dtype=jnp.int32) // RCP * CTX_DEV + every_pos
    per_group = QH // KVH
    allowed = jnp.take(mask_cols, query_pos // BLK, axis=0)
    visible = jnp.repeat(allowed, BLK, axis=1) > 0
    visible = visible & key_in_use[None, :] & (key_pos[None, :] <= query_pos[:, None])
    numerator, running, totals = attend_local(
        all_queries,
        context[:, :key_width],
        context[:, key_width:],
        visible.astype(jnp.float32),
    )
    running = jnp.transpose(running, (1, 0, 2)).reshape(query_count, QH)
    totals = jnp.transpose(totals, (1, 0, 2)).reshape(query_count, QH)
    numerator = numerator.reshape(query_count, QH, HD)
    numerator, stats = scatter_rows(
        (
            numerator.reshape(cycle_size, RCP, QH, HD),
            jnp.concatenate([running, totals], axis=-1).reshape(cycle_size, RCP, 2 * QH),
        ),
        my_ctx,
        merge_softmax,
        lambda t: (t[0].astype(jnp.bfloat16), t[1]),
        lambda t: (t[0].astype(jnp.float32), t[1]),
    )
    totals = stats[:, QH:]
    result = numerator / totals[:, :, None]
    attended = result.reshape(RCP, QH * HD).astype(jnp.bfloat16)
    return (context[None], attended[None])


def solution(mesh):
    in_specs = (
        P(("owner", "ctx"), None, None),
        P(None, "ctx"),
        P(),
        P("owner", None),
        P("owner", None, "ctx"),
        P("ctx", None),
        P("owner", "ctx", None),
        P("owner", None, "ctx"),
    )
    out_specs = (P("owner", "ctx", None), P("owner", "ctx", None))
    return jax.shard_map(
        on_device, mesh=mesh, in_specs=in_specs, out_specs=out_specs, check_vma=False
    )
```

```python
import jax
import jax.numpy as jnp
from jax import lax
from jax.experimental import pallas as pl
from jax.experimental.pallas import tpu as pltpu
from jax.sharding import PartitionSpec as P

QH = 32
KVH = 4
HD = 128
BLK = 128
NBD = 8
RCP = 8
SLOTS = 8
CAP = 4
CTX_DEV = 1024


def exchange(shard, bit):
    peers = lax.axis_size("ctx")
    return lax.ppermute(shard, "ctx", [(i, i ^ bit) for i in range(peers)])


def gather_rows(block, my_ctx):
    peers = lax.axis_size("ctx")
    held = block
    bit = 1
    while bit < peers:
        other = exchange(held, bit)
        upper = (my_ctx // bit) % 2 == 1
        held = jnp.where(
            upper, jnp.concatenate([other, held]), jnp.concatenate([held, other])
        )
        bit *= 2
    return held


def scatter_rows(parts, my_ctx, merge, narrow=lambda t: t, widen=lambda t: t):
    peers = lax.axis_size("ctx")
    held = parts
    bit = 1
    while bit < peers:
        half = jax.tree.map(lambda a: a.reshape((a.shape[0] // 2, 2) + a.shape[1:]), held)
        upper = (my_ctx // bit) % 2 == 1
        keep = jax.tree.map(lambda a: jnp.where(upper, a[:, 1], a[:, 0]), half)
        send = jax.tree.map(lambda a: jnp.where(upper, a[:, 0], a[:, 1]), half)
        held = merge(keep, widen(exchange(narrow(send), bit)))
        bit *= 2
    return jax.tree.map(lambda a: a[0], held)


def add_parts(a, b):
    return a + b


def merge_softmax(a, b):
    numerator_a, stats_a = a
    numerator_b, stats_b = b
    heads = stats_a.shape[-1] // 2
    running_a, totals_a = stats_a[..., :heads], stats_a[..., heads:]
    running_b, totals_b = stats_b[..., :heads], stats_b[..., heads:]
    newest = jnp.maximum(running_a, running_b)
    factor_a = jnp.exp(running_a - newest)
    factor_b = jnp.exp(running_b - newest)
    numerator = numerator_a * factor_a[..., None] + numerator_b * factor_b[..., None]
    totals = totals_a * factor_a + totals_b * factor_b
    return (numerator, jnp.concatenate([newest, totals], axis=-1))


def attend_kernel(query_ref, key_ref, value_ref, mask_ref, numerator_ref, running_ref, totals_ref):
    per_group = QH // KVH
    visible = mask_ref[...] > 0
    keys = key_ref[...]
    values = value_ref[...]
    for head in range(per_group):
        columns = slice(head * HD, (head + 1) * HD)
        scores = lax.dot_general(
            query_ref[:, columns],
            keys,
            (((1,), (1,)), ((), ())),
            preferred_element_type=jnp.float32,
        ) * HD ** (-0.5)
        scores = jnp.where(visible, scores, -1e30)
        highest = jnp.max(scores, axis=1, keepdims=True)
        weights = jnp.where(visible, jnp.exp(scores - highest), 0.0)
        numerator_ref[:, columns] = jnp.dot(
            weights.astype(jnp.bfloat16), values, preferred_element_type=jnp.float32
        )
        running_ref[0, :, head : head + 1] = highest
        totals_ref[0, :, head : head + 1] = jnp.sum(weights, axis=1, keepdims=True)


def attend_local(all_queries, key_rows, value_rows, visible):
    rows = all_queries.shape[0]
    keys = key_rows.shape[0]
    groups = key_rows.shape[1] // HD
    per_group = QH // KVH
    width = per_group * HD
    return pl.pallas_call(
        attend_kernel,
        grid=(groups,),
        in_specs=[
            pl.BlockSpec((rows, width), lambda k: (0, k)),
            pl.BlockSpec((keys, HD), lambda k: (0, k)),
            pl.BlockSpec((keys, HD), lambda k: (0, k)),
            pl.BlockSpec((rows, keys), lambda k: (0, 0)),
        ],
        out_specs=[
            pl.BlockSpec((rows, width), lambda k: (0, k)),
            pl.BlockSpec((1, rows, per_group), lambda k: (k, 0, 0)),
            pl.BlockSpec((1, rows, per_group), lambda k: (k, 0, 0)),
        ],
        out_shape=[
            jax.ShapeDtypeStruct((rows, groups * width), jnp.float32),
            jax.ShapeDtypeStruct((groups, rows, per_group), jnp.float32),
            jax.ShapeDtypeStruct((groups, rows, per_group), jnp.float32),
        ],
        cost_estimate=pl.CostEstimate(
            flops=4 * rows * keys * groups * width,
            transcendentals=rows * keys * groups * per_group,
            bytes_accessed=rows * groups * width * 6 + keys * groups * HD * 4 + rows * keys * 4,
        ),
    )(all_queries, key_rows, value_rows, visible)

def on_device(span_cache, retrieval, counts, recompute_pos, hidden, kv_weight, queries, block_mask):
    owner_count = lax.axis_size("owner")
    cycle_size = lax.axis_size("ctx")
    my_owner = lax.axis_index("owner")
    my_ctx = lax.axis_index("ctx")
    feature_count = span_cache.shape[2]
    positions = jnp.arange(NBD, dtype=jnp.int32)
    block_ids = my_ctx * NBD + positions
    in_use = block_ids[None, :] < counts[:, None]
    holder = retrieval // (cycle_size * SLOTS)
    outbound = in_use & (holder == my_owner)
    slot_rank = jnp.cumsum(outbound.astype(jnp.int32), axis=1) - 1
    picked = outbound[:, None, :] & (
        slot_rank[:, None, :] == jnp.arange(CAP, dtype=jnp.int32)[None, :, None]
    )
    chosen = jnp.sum(jnp.where(picked, (retrieval % SLOTS)[:, None, :], 0), axis=2)
    filled = jnp.any(picked, axis=2)
    outgoing = jnp.where(
        filled[:, :, None, None], jnp.take(span_cache, chosen, axis=0), jnp.zeros((), jnp.bfloat16)
    )
    local_rows = hidden[0]
    partial = jnp.dot(local_rows, kv_weight, preferred_element_type=jnp.float32)
    recomputed = scatter_rows(
        partial.reshape(cycle_size, RCP, feature_count), my_ctx, add_parts
    ).astype(jnp.bfloat16)
    all_queries = gather_rows(queries[0], my_ctx)
    outgoing, recomputed, all_queries = lax.optimization_barrier(
        (outgoing, recomputed, all_queries)
    )
    arrived = lax.all_to_all(outgoing, "owner", split_axis=0, concat_axis=0, tiled=True)
    wanted = lax.dynamic_index_in_dim(retrieval, my_owner, 0, keepdims=False)
    my_count = lax.dynamic_index_in_dim(counts, my_owner, 0, keepdims=False)
    my_in_use = block_ids < my_count
    source = wanted // (cycle_size * SLOTS)
    earlier = (
        (source[:, None] == source[None, :])
        & my_in_use[None, :]
        & (positions[None, :] < positions[:, None])
    )
    ordinal = jnp.sum(earlier.astype(jnp.int32), axis=1)
    flattened = arrived.reshape(owner_count * CAP, BLK, feature_count)
    blocks = jnp.take(flattened, source * CAP + ordinal, axis=0, mode="clip")
    blocks = jnp.where(my_in_use[:, None, None], blocks, jnp.zeros((), jnp.bfloat16))
    context = blocks.reshape(CTX_DEV, feature_count)
    every_pos = recompute_pos[0]
    own_pos = lax.dynamic_slice_in_dim(every_pos, my_ctx * RCP, RCP)
    matches = jnp.arange(CTX_DEV, dtype=jnp.int32)[:, None] == own_pos[None, :]
    placed = jnp.dot(
        matches.astype(jnp.bfloat16), recomputed, preferred_element_type=jnp.float32
    ).astype(jnp.bfloat16)
    context = jnp.where(jnp.any(matches, axis=1)[:, None], placed, context)
    key_width = KVH * HD
    key_pos = my_ctx * CTX_DEV + jnp.arange(CTX_DEV, dtype=jnp.int32)
    key_in_use = key_pos // BLK < my_count
    mask_cols = block_mask[0]
    query_count = cycle_size * RCP
    query_pos = jnp.arange(query_count, dtype=jnp.int32) // RCP * CTX_DEV + every_pos
    per_group = QH // KVH
    allowed = jnp.take(mask_cols, query_pos // BLK, axis=0)
    visible = jnp.repeat(allowed, BLK, axis=1) > 0
    visible = visible & key_in_use[None, :] & (key_pos[None, :] <= query_pos[:, None])
    visible = visible.astype(jnp.float32)
    halves = 2
    head_share = QH // halves
    key_share = key_width // halves
    outputs = []
    for part in range(halves):
        numerator, running, totals = attend_local(
            all_queries[:, part * head_share * HD : (part + 1) * head_share * HD],
            context[:, part * key_share : (part + 1) * key_share],
            context[:, key_width + part * key_share : key_width + (part + 1) * key_share],
            visible,
        )
        running = jnp.transpose(running, (1, 0, 2)).reshape(query_count, head_share)
        totals = jnp.transpose(totals, (1, 0, 2)).reshape(query_count, head_share)
        numerator = numerator.reshape(query_count, head_share, HD)
        numerator, stats = scatter_rows(
            (
                numerator.reshape(cycle_size, RCP, head_share, HD),
                jnp.concatenate([running, totals], axis=-1).reshape(
                    cycle_size, RCP, 2 * head_share
                ),
            ),
            my_ctx,
            merge_softmax,
            lambda t: (t[0].astype(jnp.bfloat16), t[1]),
            lambda t: (t[0].astype(jnp.float32), t[1]),
        )
        outputs.append(numerator / stats[:, head_share:, None])
    result = jnp.concatenate(outputs, axis=1)
    attended = result.reshape(RCP, QH * HD).astype(jnp.bfloat16)
    return (context[None], attended[None])


def solution(mesh):
    in_specs = (
        P(("owner", "ctx"), None, None),
        P(None, "ctx"),
        P(),
        P("owner", None),
        P("owner", None, "ctx"),
        P("ctx", None),
        P("owner", "ctx", None),
        P("owner", None, "ctx"),
    )
    out_specs = (P("owner", "ctx", None), P("owner", "ctx", None))
    return jax.shard_map(
        on_device, mesh=mesh, in_specs=in_specs, out_specs=out_specs, check_vma=False
    )
```

```python
import jax
import jax.numpy as jnp
from jax import lax
from jax.experimental import pallas as pl
from jax.experimental.pallas import tpu as pltpu
from jax.sharding import PartitionSpec as P

QH = 32
KVH = 4
HD = 128
BLK = 128
NBD = 8
RCP = 8
SLOTS = 8
CAP = 4
CTX_DEV = 1024


def exchange(shard, bit):
    peers = lax.axis_size("ctx")
    return lax.ppermute(shard, "ctx", [(i, i ^ bit) for i in range(peers)])


def gather_rows(block, my_ctx):
    peers = lax.axis_size("ctx")
    held = block
    bit = peers // 2
    while bit >= 1:
        other = exchange(held, bit)
        upper = (my_ctx // bit) % 2 == 1
        held = jnp.where(
            upper, jnp.concatenate([other, held]), jnp.concatenate([held, other])
        )
        bit //= 2
    return held


def reversed_order(peers):
    width = peers.bit_length() - 1
    return [int(format(i, "0%db" % width)[::-1], 2) for i in range(peers)]


def scatter_rows(parts, my_ctx, merge, narrow=lambda t: t, widen=lambda t: t):
    peers = lax.axis_size("ctx")
    held = parts
    bit = 1
    while bit < peers:
        half = jax.tree.map(lambda a: a.reshape((a.shape[0] // 2, 2) + a.shape[1:]), held)
        upper = (my_ctx // bit) % 2 == 1
        keep = jax.tree.map(lambda a: jnp.where(upper, a[:, 1], a[:, 0]), half)
        send = jax.tree.map(lambda a: jnp.where(upper, a[:, 0], a[:, 1]), half)
        held = merge(keep, widen(exchange(narrow(send), bit)))
        bit *= 2
    return jax.tree.map(lambda a: a[0], held)


def add_parts(a, b):
    return a + b


def merge_softmax(a, b):
    numerator_a, stats_a = a
    numerator_b, stats_b = b
    running_a, totals_a = stats_a[..., :QH], stats_a[..., QH:]
    running_b, totals_b = stats_b[..., :QH], stats_b[..., QH:]
    newest = jnp.maximum(running_a, running_b)
    factor_a = jnp.exp(running_a - newest)
    factor_b = jnp.exp(running_b - newest)
    numerator = numerator_a * factor_a[..., None] + numerator_b * factor_b[..., None]
    totals = totals_a * factor_a + totals_b * factor_b
    return (numerator, jnp.concatenate([newest, totals], axis=-1))


def attend_kernel(query_ref, key_ref, value_ref, mask_ref, numerator_ref, running_ref, totals_ref):
    per_group = QH // KVH
    visible = mask_ref[...] > 0
    keys = key_ref[...]
    values = value_ref[...]
    for head in range(per_group):
        columns = slice(head * HD, (head + 1) * HD)
        scores = lax.dot_general(
            query_ref[:, columns],
            keys,
            (((1,), (1,)), ((), ())),
            preferred_element_type=jnp.float32,
        ) * HD ** (-0.5)
        scores = jnp.where(visible, scores, -1e30)
        highest = jnp.max(scores, axis=1, keepdims=True)
        weights = jnp.where(visible, jnp.exp(scores - highest), 0.0)
        numerator_ref[:, columns] = jnp.dot(
            weights.astype(jnp.bfloat16), values, preferred_element_type=jnp.float32
        )
        running_ref[0, :, head : head + 1] = highest
        totals_ref[0, :, head : head + 1] = jnp.sum(weights, axis=1, keepdims=True)


def attend_local(all_queries, key_rows, value_rows, visible):
    rows = all_queries.shape[0]
    keys = key_rows.shape[0]
    per_group = QH // KVH
    width = per_group * HD
    return pl.pallas_call(
        attend_kernel,
        grid=(KVH,),
        in_specs=[
            pl.BlockSpec((rows, width), lambda k: (0, k)),
            pl.BlockSpec((keys, HD), lambda k: (0, k)),
            pl.BlockSpec((keys, HD), lambda k: (0, k)),
            pl.BlockSpec((rows, keys), lambda k: (0, 0)),
        ],
        out_specs=[
            pl.BlockSpec((rows, width), lambda k: (0, k)),
            pl.BlockSpec((1, rows, per_group), lambda k: (k, 0, 0)),
            pl.BlockSpec((1, rows, per_group), lambda k: (k, 0, 0)),
        ],
        out_shape=[
            jax.ShapeDtypeStruct((rows, QH * HD), jnp.float32),
            jax.ShapeDtypeStruct((KVH, rows, per_group), jnp.float32),
            jax.ShapeDtypeStruct((KVH, rows, per_group), jnp.float32),
        ],
        cost_estimate=pl.CostEstimate(
            flops=4 * rows * keys * QH * HD,
            transcendentals=rows * keys * QH,
            bytes_accessed=rows * QH * HD * 6 + keys * KVH * HD * 4 + rows * keys * 4,
        ),
    )(all_queries, key_rows, value_rows, visible)

def on_device(span_cache, retrieval, counts, recompute_pos, hidden, kv_weight, queries, block_mask):
    owner_count = lax.axis_size("owner")
    cycle_size = lax.axis_size("ctx")
    my_owner = lax.axis_index("owner")
    my_ctx = lax.axis_index("ctx")
    feature_count = span_cache.shape[2]
    positions = jnp.arange(NBD, dtype=jnp.int32)
    block_ids = my_ctx * NBD + positions
    in_use = block_ids[None, :] < counts[:, None]
    holder = retrieval // (cycle_size * SLOTS)
    outbound = in_use & (holder == my_owner)
    slot_rank = jnp.cumsum(outbound.astype(jnp.int32), axis=1) - 1
    picked = outbound[:, None, :] & (
        slot_rank[:, None, :] == jnp.arange(CAP, dtype=jnp.int32)[None, :, None]
    )
    chosen = jnp.sum(jnp.where(picked, (retrieval % SLOTS)[:, None, :], 0), axis=2)
    filled = jnp.any(picked, axis=2)
    outgoing = jnp.where(
        filled[:, :, None, None], jnp.take(span_cache, chosen, axis=0), jnp.zeros((), jnp.bfloat16)
    )
    local_rows = hidden[0]
    partial = jnp.dot(local_rows, kv_weight, preferred_element_type=jnp.float32)
    recomputed = scatter_rows(
        partial.reshape(cycle_size, RCP, feature_count), my_ctx, add_parts
    ).astype(jnp.bfloat16)
    all_queries = gather_rows(queries[0], my_ctx)
    outgoing, recomputed, all_queries = lax.optimization_barrier(
        (outgoing, recomputed, all_queries)
    )
    all_queries = all_queries.reshape(cycle_size, RCP, QH * HD)[
        jnp.array(reversed_order(cycle_size))
    ].reshape(cycle_size * RCP, QH * HD)
    arrived = lax.all_to_all(outgoing, "owner", split_axis=0, concat_axis=0, tiled=True)
    wanted = lax.dynamic_index_in_dim(retrieval, my_owner, 0, keepdims=False)
    my_count = lax.dynamic_index_in_dim(counts, my_owner, 0, keepdims=False)
    my_in_use = block_ids < my_count
    source = wanted // (cycle_size * SLOTS)
    earlier = (
        (source[:, None] == source[None, :])
        & my_in_use[None, :]
        & (positions[None, :] < positions[:, None])
    )
    ordinal = jnp.sum(earlier.astype(jnp.int32), axis=1)
    flattened = arrived.reshape(owner_count * CAP, BLK, feature_count)
    blocks = jnp.take(flattened, source * CAP + ordinal, axis=0, mode="clip")
    blocks = jnp.where(my_in_use[:, None, None], blocks, jnp.zeros((), jnp.bfloat16))
    context = blocks.reshape(CTX_DEV, feature_count)
    every_pos = recompute_pos[0]
    own_pos = lax.dynamic_slice_in_dim(every_pos, my_ctx * RCP, RCP)
    matches = jnp.arange(CTX_DEV, dtype=jnp.int32)[:, None] == own_pos[None, :]
    placed = jnp.dot(
        matches.astype(jnp.bfloat16), recomputed, preferred_element_type=jnp.float32
    ).astype(jnp.bfloat16)
    context = jnp.where(jnp.any(matches, axis=1)[:, None], placed, context)
    key_width = KVH * HD
    key_pos = my_ctx * CTX_DEV + jnp.arange(CTX_DEV, dtype=jnp.int32)
    key_in_use = key_pos // BLK < my_count
    mask_cols = block_mask[0]
    query_count = cycle_size * RCP
    query_pos = jnp.arange(query_count, dtype=jnp.int32) // RCP * CTX_DEV + every_pos
    per_group = QH // KVH
    allowed = jnp.take(mask_cols, query_pos // BLK, axis=0)
    visible = jnp.repeat(allowed, BLK, axis=1) > 0
    visible = visible & key_in_use[None, :] & (key_pos[None, :] <= query_pos[:, None])
    numerator, running, totals = attend_local(
        all_queries,
        context[:, :key_width],
        context[:, key_width:],
        visible.astype(jnp.float32),
    )
    running = jnp.transpose(running, (1, 0, 2)).reshape(query_count, QH)
    totals = jnp.transpose(totals, (1, 0, 2)).reshape(query_count, QH)
    numerator = numerator.reshape(query_count, QH, HD)
    numerator, stats = scatter_rows(
        (
            numerator.reshape(cycle_size, RCP, QH, HD),
            jnp.concatenate([running, totals], axis=-1).reshape(cycle_size, RCP, 2 * QH),
        ),
        my_ctx,
        merge_softmax,
        lambda t: (t[0].astype(jnp.bfloat16), t[1]),
        lambda t: (t[0].astype(jnp.float32), t[1]),
    )
    totals = stats[:, QH:]
    result = numerator / totals[:, :, None]
    attended = result.reshape(RCP, QH * HD).astype(jnp.bfloat16)
    return (context[None], attended[None])


def solution(mesh):
    in_specs = (
        P(("owner", "ctx"), None, None),
        P(None, "ctx"),
        P(),
        P("owner", None),
        P("owner", None, "ctx"),
        P("ctx", None),
        P("owner", "ctx", None),
        P("owner", None, "ctx"),
    )
    out_specs = (P("owner", "ctx", None), P("owner", "ctx", None))
    return jax.shard_map(
        on_device, mesh=mesh, in_specs=in_specs, out_specs=out_specs, check_vma=False
    )
```

```python
import jax
import jax.numpy as jnp
from jax import lax
from jax.experimental import pallas as pl
from jax.experimental.pallas import tpu as pltpu
from jax.sharding import PartitionSpec as P

QH = 32
KVH = 4
HD = 128
BLK = 128
NBD = 8
RCP = 8
SLOTS = 8
CAP = 4
CTX_DEV = 1024


def exchange(shard, bit):
    peers = lax.axis_size("ctx")
    return lax.ppermute(shard, "ctx", [(i, i ^ bit) for i in range(peers)])


def gather_rows(block, my_ctx, rider):
    peers = lax.axis_size("ctx")
    held = block
    bit = peers // 2
    while bit >= 1:
        other = exchange(held, bit)
        if rider is not None:
            other, rider = lax.optimization_barrier((other, rider))
        upper = (my_ctx // bit) % 2 == 1
        held = jnp.where(
            upper, jnp.concatenate([other, held]), jnp.concatenate([held, other])
        )
        bit //= 2
        if bit * 2 == peers // 2:
            result_rider, rider = rider, None
    return held, result_rider


def reversed_order(peers):
    width = peers.bit_length() - 1
    return [int(format(i, "0%db" % width)[::-1], 2) for i in range(peers)]


def scatter_rows(parts, my_ctx, merge, narrow=lambda t: t, widen=lambda t: t):
    peers = lax.axis_size("ctx")
    held = parts
    bit = 1
    while bit < peers:
        half = jax.tree.map(lambda a: a.reshape((a.shape[0] // 2, 2) + a.shape[1:]), held)
        upper = (my_ctx // bit) % 2 == 1
        keep = jax.tree.map(lambda a: jnp.where(upper, a[:, 1], a[:, 0]), half)
        send = jax.tree.map(lambda a: jnp.where(upper, a[:, 0], a[:, 1]), half)
        held = merge(keep, widen(exchange(narrow(send), bit)))
        bit *= 2
    return jax.tree.map(lambda a: a[0], held)


def add_parts(a, b):
    return a + b


def merge_softmax(a, b):
    numerator_a, stats_a = a
    numerator_b, stats_b = b
    running_a, totals_a = stats_a[..., :QH], stats_a[..., QH:]
    running_b, totals_b = stats_b[..., :QH], stats_b[..., QH:]
    newest = jnp.maximum(running_a, running_b)
    factor_a = jnp.exp(running_a - newest)
    factor_b = jnp.exp(running_b - newest)
    numerator = numerator_a * factor_a[..., None] + numerator_b * factor_b[..., None]
    totals = totals_a * factor_a + totals_b * factor_b
    return (numerator, jnp.concatenate([newest, totals], axis=-1))


def attend_kernel(query_ref, key_ref, value_ref, mask_ref, numerator_ref, running_ref, totals_ref):
    per_group = QH // KVH
    visible = mask_ref[...] > 0
    keys = key_ref[...]
    values = value_ref[...]
    for head in range(per_group):
        columns = slice(head * HD, (head + 1) * HD)
        scores = lax.dot_general(
            query_ref[:, columns],
            keys,
            (((1,), (1,)), ((), ())),
            preferred_element_type=jnp.float32,
        ) * HD ** (-0.5)
        scores = jnp.where(visible, scores, -1e30)
        highest = jnp.max(scores, axis=1, keepdims=True)
        weights = jnp.where(visible, jnp.exp(scores - highest), 0.0)
        numerator_ref[:, columns] = jnp.dot(
            weights.astype(jnp.bfloat16), values, preferred_element_type=jnp.float32
        )
        running_ref[0, :, head : head + 1] = highest
        totals_ref[0, :, head : head + 1] = jnp.sum(weights, axis=1, keepdims=True)


def attend_local(all_queries, key_rows, value_rows, visible):
    rows = all_queries.shape[0]
    keys = key_rows.shape[0]
    per_group = QH // KVH
    width = per_group * HD
    return pl.pallas_call(
        attend_kernel,
        grid=(KVH,),
        in_specs=[
            pl.BlockSpec((rows, width), lambda k: (0, k)),
            pl.BlockSpec((keys, HD), lambda k: (0, k)),
            pl.BlockSpec((keys, HD), lambda k: (0, k)),
            pl.BlockSpec((rows, keys), lambda k: (0, 0)),
        ],
        out_specs=[
            pl.BlockSpec((rows, width), lambda k: (0, k)),
            pl.BlockSpec((1, rows, per_group), lambda k: (k, 0, 0)),
            pl.BlockSpec((1, rows, per_group), lambda k: (k, 0, 0)),
        ],
        out_shape=[
            jax.ShapeDtypeStruct((rows, QH * HD), jnp.float32),
            jax.ShapeDtypeStruct((KVH, rows, per_group), jnp.float32),
            jax.ShapeDtypeStruct((KVH, rows, per_group), jnp.float32),
        ],
        cost_estimate=pl.CostEstimate(
            flops=4 * rows * keys * QH * HD,
            transcendentals=rows * keys * QH,
            bytes_accessed=rows * QH * HD * 6 + keys * KVH * HD * 4 + rows * keys * 4,
        ),
    )(all_queries, key_rows, value_rows, visible)

def on_device(span_cache, retrieval, counts, recompute_pos, hidden, kv_weight, queries, block_mask):
    owner_count = lax.axis_size("owner")
    cycle_size = lax.axis_size("ctx")
    my_owner = lax.axis_index("owner")
    my_ctx = lax.axis_index("ctx")
    feature_count = span_cache.shape[2]
    positions = jnp.arange(NBD, dtype=jnp.int32)
    block_ids = my_ctx * NBD + positions
    in_use = block_ids[None, :] < counts[:, None]
    holder = retrieval // (cycle_size * SLOTS)
    outbound = in_use & (holder == my_owner)
    slot_rank = jnp.cumsum(outbound.astype(jnp.int32), axis=1) - 1
    picked = outbound[:, None, :] & (
        slot_rank[:, None, :] == jnp.arange(CAP, dtype=jnp.int32)[None, :, None]
    )
    chosen = jnp.sum(jnp.where(picked, (retrieval % SLOTS)[:, None, :], 0), axis=2)
    filled = jnp.any(picked, axis=2)
    outgoing = jnp.where(
        filled[:, :, None, None], jnp.take(span_cache, chosen, axis=0), jnp.zeros((), jnp.bfloat16)
    )
    local_rows = hidden[0]
    partial = jnp.dot(local_rows, kv_weight, preferred_element_type=jnp.float32)
    recomputed = scatter_rows(
        partial.reshape(cycle_size, RCP, feature_count), my_ctx, add_parts
    ).astype(jnp.bfloat16)
    all_queries, outgoing = gather_rows(queries[0], my_ctx, outgoing)
    outgoing, recomputed, all_queries = lax.optimization_barrier(
        (outgoing, recomputed, all_queries)
    )
    all_queries = all_queries.reshape(cycle_size, RCP, QH * HD)[
        jnp.array(reversed_order(cycle_size))
    ].reshape(cycle_size * RCP, QH * HD)
    arrived = lax.all_to_all(outgoing, "owner", split_axis=0, concat_axis=0, tiled=True)
    wanted = lax.dynamic_index_in_dim(retrieval, my_owner, 0, keepdims=False)
    my_count = lax.dynamic_index_in_dim(counts, my_owner, 0, keepdims=False)
    my_in_use = block_ids < my_count
    source = wanted // (cycle_size * SLOTS)
    earlier = (
        (source[:, None] == source[None, :])
        & my_in_use[None, :]
        & (positions[None, :] < positions[:, None])
    )
    ordinal = jnp.sum(earlier.astype(jnp.int32), axis=1)
    flattened = arrived.reshape(owner_count * CAP, BLK, feature_count)
    blocks = jnp.take(flattened, source * CAP + ordinal, axis=0, mode="clip")
    blocks = jnp.where(my_in_use[:, None, None], blocks, jnp.zeros((), jnp.bfloat16))
    context = blocks.reshape(CTX_DEV, feature_count)
    every_pos = recompute_pos[0]
    own_pos = lax.dynamic_slice_in_dim(every_pos, my_ctx * RCP, RCP)
    matches = jnp.arange(CTX_DEV, dtype=jnp.int32)[:, None] == own_pos[None, :]
    placed = jnp.dot(
        matches.astype(jnp.bfloat16), recomputed, preferred_element_type=jnp.float32
    ).astype(jnp.bfloat16)
    context = jnp.where(jnp.any(matches, axis=1)[:, None], placed, context)
    key_width = KVH * HD
    key_pos = my_ctx * CTX_DEV + jnp.arange(CTX_DEV, dtype=jnp.int32)
    key_in_use = key_pos // BLK < my_count
    mask_cols = block_mask[0]
    query_count = cycle_size * RCP
    query_pos = jnp.arange(query_count, dtype=jnp.int32) // RCP * CTX_DEV + every_pos
    per_group = QH // KVH
    allowed = jnp.take(mask_cols, query_pos // BLK, axis=0)
    visible = jnp.repeat(allowed, BLK, axis=1) > 0
    visible = visible & key_in_use[None, :] & (key_pos[None, :] <= query_pos[:, None])
    numerator, running, totals = attend_local(
        all_queries,
        context[:, :key_width],
        context[:, key_width:],
        visible.astype(jnp.float32),
    )
    running = jnp.transpose(running, (1, 0, 2)).reshape(query_count, QH)
    totals = jnp.transpose(totals, (1, 0, 2)).reshape(query_count, QH)
    numerator = numerator.reshape(query_count, QH, HD)
    numerator, stats = scatter_rows(
        (
            numerator.reshape(cycle_size, RCP, QH, HD),
            jnp.concatenate([running, totals], axis=-1).reshape(cycle_size, RCP, 2 * QH),
        ),
        my_ctx,
        merge_softmax,
        lambda t: (t[0].astype(jnp.bfloat16), t[1]),
        lambda t: (t[0].astype(jnp.float32), t[1]),
    )
    totals = stats[:, QH:]
    result = numerator / totals[:, :, None]
    attended = result.reshape(RCP, QH * HD).astype(jnp.bfloat16)
    return (context[None], attended[None])


def solution(mesh):
    in_specs = (
        P(("owner", "ctx"), None, None),
        P(None, "ctx"),
        P(),
        P("owner", None),
        P("owner", None, "ctx"),
        P("ctx", None),
        P("owner", "ctx", None),
        P("owner", None, "ctx"),
    )
    out_specs = (P("owner", "ctx", None), P("owner", "ctx", None))
    return jax.shard_map(
        on_device, mesh=mesh, in_specs=in_specs, out_specs=out_specs, check_vma=False
    )
```
